256 devices in a mesh: gz: 32 (over z, y_hi, core), ch: 8 (over y_lo, x).
Axes of the slice: x: 4, y: 4 (y_hi: 2, y_lo: 2; y = y_hi * 2 + y_lo), z: 8, core: 2. Of those that a mesh axis runs over, the one named last changes fastest.
Arguments:
- volume: bfloat16 [64, 1024, 512], P('ch', 'gz'), may hold values from -6 to 6
- plane_a: bfloat16 [2, 64, 64, 3, 3], P(None, 'ch'), may hold values from -0.375 to 0.375
- plane_b: bfloat16 [2, 64, 64, 3, 3], P(None, 'ch'), may hold values from -0.375 to 0.375
- depth: bfloat16 [2, 64, 64, 3], P(None, 'ch'), may hold values from -0.625 to 0.625
Outputs:
- features: bfloat16 [64, 1024, 512], P('ch', 'gz')
The draws below stay inside these ranges and needn't reach their ends.
All inputs are finite; a program needn't handle non-finite values.
Results may differ from the reference program's by a relative error of at most 0.015.
Values may be sent and summed in bfloat16 or wider, within the bound.
No kernel may reach another device: no remote copies, remote signals or barrier semaphores. Data moves between devices by JAX's collectives and lax.ppermute only.
A program may use at most 64 MiB of HBM per device.

```python
import jax
import jax.numpy as jnp
from jax import lax

C = 64
X = 64
Y = 8
DEPTH_DILATION = 64
LAYERS = 2
Z = 1024


def levels(own_key, extent, shards, smallest, high):
    factor_of, own = 1.0, jax.random.fold_in(own_key, 6)
    for axis_at, parts in shards:
        heights = jnp.exp(jax.random.uniform(jax.random.fold_in(own, axis_at), (parts,), jnp.float32, smallest / len(shards), high / len(shards)))
        factor_of = factor_of * jnp.repeat(heights, extent[axis_at] // parts).reshape([-1 if axis == axis_at else 1 for axis in range(len(extent))])
    return factor_of


def gaussian(rng, dims, width, most, pieces=(), dtype=jnp.bfloat16):
    result = width * jax.random.normal(rng, dims, jnp.float32)
    if pieces:
        result = result * levels(rng, dims, pieces, -0.22, 0.18)
    return jnp.clip(result, -most, most).astype(dtype)


def setup_inputs(seed: int = 0) -> dict:
    key_of = jax.random.split(jax.random.key(seed), 5)
    volume = gaussian(key_of[0], (C, Z, X * Y), 1.0, 6.0, ((0, 8), (1, 32)))
    plane_a = gaussian(key_of[1], (LAYERS, C, C, 3, 3), (C * 9 // 2) ** -0.5, 0.375, ((1, 8),))
    plane_b = gaussian(key_of[2], (LAYERS, C, C, 3, 3), (C * 9 // 2) ** -0.5, 0.375, ((1, 8),))
    depth = gaussian(key_of[3], (LAYERS, C, C, 3), (C * 3 // 2) ** -0.5, 0.625, ((1, 8),))
    return {"volume": volume, "plane_a": plane_a, "plane_b": plane_b, "depth": depth}


def convolve_layer(running_state, filter_weight, padding, dilation_factor):
    out = lax.conv_general_dilated(running_state.astype(jnp.float32), filter_weight.astype(jnp.float32), (1, 1, 1), padding, rhs_dilation=dilation_factor, dimension_numbers=("NCDHW", "OIDHW", "NCDHW"), precision=lax.Precision.HIGHEST)
    return jnp.maximum(out, 0.0).astype(jnp.bfloat16)


def reference(volume, plane_a, plane_b, depth):
    running_state = volume.reshape(1, C, Z, X, Y)
    flat_pad = ((0, 0), (1, 1), (1, 1))
    for layer_index in range(LAYERS):
        running_state = convolve_layer(running_state, plane_a[layer_index][:, :, None], flat_pad, (1, 1, 1))
        running_state = convolve_layer(running_state, plane_b[layer_index][:, :, None], flat_pad, (1, 1, 1))
        running_state = convolve_layer(running_state, depth[layer_index][:, :, :, None, None], ((DEPTH_DILATION, DEPTH_DILATION), (0, 0), (0, 0)), (DEPTH_DILATION, 1, 1))
    return running_state.reshape(C, Z, X * Y)
```

```python
import jax
import jax.numpy as jnp
from jax import lax
from jax.sharding import PartitionSpec as P

X = 64
Y = 8


def from_behind(block, axis, distance):
    devices = range(lax.axis_size(axis))
    route = [(i - distance, i) for i in devices if i - distance in devices]
    return lax.ppermute(block, axis, route)


def gather_weights(plane_a, plane_b, depth):
    layers, out_part, chans = plane_a.shape[:3]
    packed = jnp.concatenate(
        [
            plane_a.reshape(layers, out_part, -1),
            plane_b.reshape(layers, out_part, -1),
            depth.reshape(layers, out_part, -1),
        ],
        axis=2,
    )
    packed = lax.all_gather(packed, "ch", axis=1, tiled=True)
    cut_a = chans * 9
    full_a = packed[:, :, :cut_a].reshape(layers, -1, chans, 3, 3)
    full_b = packed[:, :, cut_a : 2 * cut_a].reshape(layers, -1, chans, 3, 3)
    full_d = packed[:, :, 2 * cut_a :].reshape(layers, -1, chans, 3)
    return full_a, full_b, full_d


def plane_conv(h, weight):
    out = lax.conv_general_dilated(
        h,
        weight,
        (1, 1),
        ((1, 1), (1, 1)),
        dimension_numbers=("CNHW", "OIHW", "CNHW"),
        preferred_element_type=jnp.float32,
    )
    return jnp.maximum(out, 0.0).astype(jnp.bfloat16)


def depth_conv(second, weight):
    lower = from_behind(second, "gz", 2)
    upper = from_behind(second, "gz", -2)
    total = jnp.einsum("oi,isxy->osxy", weight[:, :, 1], second, preferred_element_type=jnp.float32)
    total = total + jnp.einsum("oi,isxy->osxy", weight[:, :, 0], lower, preferred_element_type=jnp.float32)
    total = total + jnp.einsum("oi,isxy->osxy", weight[:, :, 2], upper, preferred_element_type=jnp.float32)
    return jnp.maximum(total, 0.0).astype(jnp.bfloat16)


def local(volume, plane_a, plane_b, depth):
    full_a, full_b, full_d = gather_weights(plane_a, plane_b, depth)
    part, slab, flat = volume.shape
    h = lax.all_to_all(volume, "ch", split_axis=1, concat_axis=0, tiled=True)
    chans, slices = h.shape[:2]
    h = h.reshape(chans, slices, X, Y)
    for layer_index in range(plane_a.shape[0]):
        first = plane_conv(h, full_a[layer_index])
        second = plane_conv(first, full_b[layer_index])
        h = depth_conv(second, full_d[layer_index])
    h = h.reshape(chans, slices, flat)
    return lax.all_to_all(h, "ch", split_axis=0, concat_axis=1, tiled=True)


def solution(mesh):
    return jax.shard_map(
        local,
        mesh=mesh,
        in_specs=(
            P("ch", "gz", None),
            P(None, "ch", None, None, None),
            P(None, "ch", None, None, None),
            P(None, "ch", None, None),
        ),
        out_specs=P("ch", "gz", None),
        check_vma=False,
    )
```

```python
import jax
import jax.numpy as jnp
from jax import lax
from jax.sharding import PartitionSpec as P

X = 64
Y = 8


def from_behind(block, axis, distance):
    devices = range(lax.axis_size(axis))
    route = [(i - distance, i) for i in devices if i - distance in devices]
    return lax.ppermute(block, axis, route)


def gather_weights(plane_a, plane_b, depth):
    return (
        lax.all_gather(plane_a, "ch", axis=1, tiled=True),
        lax.all_gather(plane_b, "ch", axis=1, tiled=True),
        lax.all_gather(depth, "ch", axis=1, tiled=True),
    )


def plane_conv(h, weight):
    out = lax.conv_general_dilated(
        h,
        weight,
        (1, 1),
        ((1, 1), (1, 1)),
        dimension_numbers=("CNHW", "OIHW", "CNHW"),
        preferred_element_type=jnp.float32,
    )
    return jnp.maximum(out, 0.0).astype(jnp.bfloat16)


def depth_conv(second, weight):
    lower = from_behind(second, "gz", 2)
    upper = from_behind(second, "gz", -2)
    total = jnp.einsum("oi,isxy->osxy", weight[:, :, 1], second, preferred_element_type=jnp.float32)
    total = total + jnp.einsum("oi,isxy->osxy", weight[:, :, 0], lower, preferred_element_type=jnp.float32)
    total = total + jnp.einsum("oi,isxy->osxy", weight[:, :, 2], upper, preferred_element_type=jnp.float32)
    return jnp.maximum(total, 0.0).astype(jnp.bfloat16)


def local(volume, plane_a, plane_b, depth):
    full_a, full_b, full_d = gather_weights(plane_a, plane_b, depth)
    part, slab, flat = volume.shape
    h = lax.all_to_all(volume, "ch", split_axis=1, concat_axis=0, tiled=True)
    chans, slices = h.shape[:2]
    h = h.reshape(chans, slices, X, Y)
    for layer_index in range(plane_a.shape[0]):
        first = plane_conv(h, full_a[layer_index])
        second = plane_conv(first, full_b[layer_index])
        h = depth_conv(second, full_d[layer_index])
    h = h.reshape(chans, slices, flat)
    return lax.all_to_all(h, "ch", split_axis=0, concat_axis=1, tiled=True)


def solution(mesh):
    return jax.shard_map(
        local,
        mesh=mesh,
        in_specs=(
            P("ch", "gz", None),
            P(None, "ch", None, None, None),
            P(None, "ch", None, None, None),
            P(None, "ch", None, None),
        ),
        out_specs=P("ch", "gz", None),
        check_vma=False,
    )
```

```python
import jax
import jax.numpy as jnp
from jax import lax
from jax.sharding import PartitionSpec as P

X = 64
Y = 8


def from_behind(block, axis, distance):
    devices = range(lax.axis_size(axis))
    route = [(i - distance, i) for i in devices if i - distance in devices]
    return lax.ppermute(block, axis, route)


def plane_conv(h, weight):
    out = lax.conv_general_dilated(
        h,
        weight,
        (1, 1),
        ((1, 1), (1, 1)),
        dimension_numbers=("CNHW", "OIHW", "CNHW"),
        preferred_element_type=jnp.float32,
    )
    return jnp.maximum(out, 0.0).astype(jnp.bfloat16)


def depth_conv(second, weight):
    lower = from_behind(second, "gz", 2)
    upper = from_behind(second, "gz", -2)
    total = jnp.einsum("oi,isxy->osxy", weight[:, :, 1], second, preferred_element_type=jnp.float32)
    total = total + jnp.einsum("oi,isxy->osxy", weight[:, :, 0], lower, preferred_element_type=jnp.float32)
    total = total + jnp.einsum("oi,isxy->osxy", weight[:, :, 2], upper, preferred_element_type=jnp.float32)
    return jnp.maximum(total, 0.0).astype(jnp.bfloat16)


def pack_weights(plane_a, plane_b, depth):
    layers, out_part, chans = plane_a.shape[:3]
    taps_a = jnp.transpose(plane_a, (0, 3, 4, 1, 2)).reshape(-1, out_part, chans)
    taps_b = jnp.transpose(plane_b, (0, 3, 4, 1, 2)).reshape(-1, out_part, chans)
    taps_d = jnp.transpose(depth, (0, 3, 1, 2)).reshape(-1, out_part, chans)
    return jnp.concatenate([taps_a, taps_b, taps_d], axis=0)


def local(volume, plane_a, plane_b, depth):
    layers, out_part, chans = plane_a.shape[:3]
    part, slab, flat = volume.shape
    parts = lax.axis_size("ch")
    slices = slab // parts
    weights = pack_weights(plane_a, plane_b, depth)
    taps = weights.shape[0]
    sent_volume = jnp.transpose(volume.reshape(part, parts, slices, flat), (1, 0, 2, 3))
    sent_volume = sent_volume.reshape(parts, part * slices, flat)
    sent_weights = jnp.broadcast_to(
        weights.reshape(1, -1, flat), (parts, taps * out_part * chans // flat, flat)
    )
    sent = jnp.concatenate([sent_volume, sent_weights], axis=1)
    got = lax.all_to_all(sent, "ch", split_axis=0, concat_axis=0, tiled=True)
    got = got.reshape(parts, -1, flat)
    h = got[:, : part * slices].reshape(parts * part, slices, X, Y)
    w = got[:, part * slices :].reshape(parts, taps, out_part, chans)
    w = jnp.transpose(w, (1, 0, 2, 3)).reshape(taps, parts * out_part, chans)
    nine = 9 * layers
    full_a = w[:nine].reshape(layers, 3, 3, parts * out_part, chans).transpose(0, 3, 4, 1, 2)
    full_b = w[nine : 2 * nine].reshape(layers, 3, 3, parts * out_part, chans).transpose(0, 3, 4, 1, 2)
    full_d = w[2 * nine :].reshape(layers, 3, parts * out_part, chans).transpose(0, 2, 3, 1)
    for layer_index in range(layers):
        first = plane_conv(h, full_a[layer_index])
        second = plane_conv(first, full_b[layer_index])
        h = depth_conv(second, full_d[layer_index])
    h = h.reshape(parts * part, slices, flat)
    return lax.all_to_all(h, "ch", split_axis=0, concat_axis=1, tiled=True)


def solution(mesh):
    return jax.shard_map(
        local,
        mesh=mesh,
        in_specs=(
            P("ch", "gz", None),
            P(None, "ch", None, None, None),
            P(None, "ch", None, None, None),
            P(None, "ch", None, None),
        ),
        out_specs=P("ch", "gz", None),
        check_vma=False,
    )
```

```python
import functools

import jax
import jax.numpy as jnp
from jax import lax
from jax.experimental import pallas as pl
from jax.experimental.pallas import tpu as pltpu
from jax.sharding import PartitionSpec as P

X = 64
Y = 8


def from_behind(block, axis, distance):
    devices = range(lax.axis_size(axis))
    route = [(i - distance, i) for i in devices if i - distance in devices]
    return lax.ppermute(block, axis, route)


def pack_weights(plane_a, plane_b, depth):
    layers, out_part, chans = plane_a.shape[:3]
    taps_a = jnp.transpose(plane_a, (0, 3, 4, 1, 2)).reshape(-1, out_part, chans)
    taps_b = jnp.transpose(plane_b, (0, 3, 4, 1, 2)).reshape(-1, out_part, chans)
    taps_d = jnp.transpose(depth, (0, 3, 1, 2)).reshape(-1, out_part, chans)
    return jnp.concatenate([taps_a, taps_b, taps_d], axis=0)


def _plane(x, w_ref, base, ok):
    total = None
    width = x.shape[1]
    for a in range(3):
        for b in range(3):
            term = jnp.dot(w_ref[base + a * 3 + b], x, preferred_element_type=jnp.float32)
            d = (a - 1) * Y + (b - 1)
            if d != 0:
                term = pltpu.roll(term, (-d) % width, 1)
            mask = ok[a][b]
            if mask is not None:
                term = jnp.where(mask, term, 0.0)
            total = term if total is None else total + term
    return total


def _masks(width):
    p = lax.broadcasted_iota(jnp.int32, (1, width), 1)
    yy = p % Y
    xx = (p // Y) % X
    xm = [xx >= 1, None, xx <= X - 2]
    ym = [yy >= 1, None, yy <= Y - 2]
    ok = []
    for a in range(3):
        row = []
        for b in range(3):
            if xm[a] is None:
                row.append(ym[b])
            elif ym[b] is None:
                row.append(xm[a])
            else:
                row.append(jnp.logical_and(xm[a], ym[b]))
        ok.append(row)
    return ok


def _kernel(*refs, depth_base, plane_bases):
    if depth_base is None:
        x_ref, w_ref, o_ref = refs
        h = x_ref[...]
    else:
        lo_ref, mid_ref, up_ref, w_ref, o_ref = refs
        total = jnp.dot(w_ref[depth_base + 1], mid_ref[...], preferred_element_type=jnp.float32)
        total = total + jnp.dot(w_ref[depth_base], lo_ref[...], preferred_element_type=jnp.float32)
        total = total + jnp.dot(w_ref[depth_base + 2], up_ref[...], preferred_element_type=jnp.float32)
        h = jnp.maximum(total, 0.0).astype(jnp.bfloat16)
    if plane_bases:
        ok = _masks(h.shape[1])
        for base in plane_bases:
            h = jnp.maximum(_plane(h, w_ref, base, ok), 0.0).astype(jnp.bfloat16)
    o_ref[...] = h


def layer_kernel(inputs, w, depth_base=None, plane_bases=()):
    shape = inputs[0].shape
    return pl.pallas_call(
        functools.partial(_kernel, depth_base=depth_base, plane_bases=tuple(plane_bases)),
        out_shape=jax.ShapeDtypeStruct(shape, jnp.bfloat16),
    )(*inputs, w)


def local(volume, plane_a, plane_b, depth):
    layers, out_part, chans = plane_a.shape[:3]
    part, slab, flat = volume.shape
    parts = lax.axis_size("ch")
    slices = slab // parts
    weights = pack_weights(plane_a, plane_b, depth)
    taps = weights.shape[0]
    sent_volume = jnp.transpose(volume.reshape(part, parts, slices, flat), (1, 0, 2, 3))
    sent_volume = sent_volume.reshape(parts, part * slices, flat)
    sent_weights = jnp.broadcast_to(
        weights.reshape(1, -1, flat), (parts, taps * out_part * chans // flat, flat)
    )
    sent = jnp.concatenate([sent_volume, sent_weights], axis=1)
    got = lax.all_to_all(sent, "ch", split_axis=0, concat_axis=0, tiled=True)
    got = got.reshape(parts, -1, flat)
    h = got[:, : part * slices].reshape(parts * part, slices * flat)
    w = got[:, part * slices :].reshape(parts, taps, out_part, chans)
    w = jnp.transpose(w, (1, 0, 2, 3)).reshape(taps, parts * out_part, chans)
    nine = 9 * layers

    def bases(layer_index):
        return (layer_index * 9, nine + layer_index * 9)

    second = layer_kernel([h], w, None, bases(0))
    for layer_index in range(layers):
        lower = from_behind(second, "gz", 2)
        upper = from_behind(second, "gz", -2)
        following = bases(layer_index + 1) if layer_index + 1 < layers else ()
        second = layer_kernel(
            [lower, second, upper], w, 2 * nine + layer_index * 3, following
        )
    h = second.reshape(parts * part, slices, flat)
    return lax.all_to_all(h, "ch", split_axis=0, concat_axis=1, tiled=True)


def solution(mesh):
    return jax.shard_map(
        local,
        mesh=mesh,
        in_specs=(
            P("ch", "gz", None),
            P(None, "ch", None, None, None),
            P(None, "ch", None, None, None),
            P(None, "ch", None, None),
        ),
        out_specs=P("ch", "gz", None),
        check_vma=False,
    )
```

```python
import functools

import jax
import jax.numpy as jnp
from jax import lax
from jax.experimental import pallas as pl
from jax.experimental.pallas import tpu as pltpu
from jax.sharding import PartitionSpec as P

X = 64
Y = 8


def from_behind(block, distance, swap):
    slabs, parts = lax.axis_size("gz"), lax.axis_size("ch")
    route = [
        ((g - distance) * parts + (c ^ swap), g * parts + c)
        for g in range(slabs)
        if 0 <= g - distance < slabs
        for c in range(parts)
    ]
    return lax.ppermute(block, ("gz", "ch"), route)


def swap_halves(block, axis, flag):
    shape = block.shape
    halves = block.reshape(shape[:axis] + (2, shape[axis] // 2) + shape[axis + 1 :])
    swapped = jnp.flip(halves, axis)
    return jnp.where(flag, swapped, halves).reshape(shape)


def pack_weights(plane_a, plane_b, depth):
    layers, out_part, chans = plane_a.shape[:3]
    taps_a = jnp.transpose(plane_a, (0, 3, 4, 1, 2)).reshape(-1, out_part, chans)
    taps_b = jnp.transpose(plane_b, (0, 3, 4, 1, 2)).reshape(-1, out_part, chans)
    taps_d = jnp.transpose(depth, (0, 3, 1, 2)).reshape(-1, out_part, chans)
    return jnp.concatenate([taps_a, taps_b, taps_d], axis=0)


def _plane(x, w_ref, base, ok):
    total = None
    width = x.shape[1]
    for a in range(3):
        for b in range(3):
            term = jnp.dot(w_ref[base + a * 3 + b], x, preferred_element_type=jnp.float32)
            d = (a - 1) * Y + (b - 1)
            if d != 0:
                term = pltpu.roll(term, (-d) % width, 1)
            mask = ok[a][b]
            if mask is not None:
                term = jnp.where(mask, term, 0.0)
            total = term if total is None else total + term
    return total


def _masks(width):
    p = lax.broadcasted_iota(jnp.int32, (1, width), 1)
    yy = p % Y
    xx = (p // Y) % X
    xm = [xx >= 1, None, xx <= X - 2]
    ym = [yy >= 1, None, yy <= Y - 2]
    ok = []
    for a in range(3):
        row = []
        for b in range(3):
            if xm[a] is None:
                row.append(ym[b])
            elif ym[b] is None:
                row.append(xm[a])
            else:
                row.append(jnp.logical_and(xm[a], ym[b]))
        ok.append(row)
    return ok


def _kernel(*refs, depth_base, plane_bases):
    if depth_base is None:
        x_ref, w_ref, o_ref = refs
        h = x_ref[...]
    else:
        lo_ref, mid_ref, up_ref, w_ref, o_ref = refs
        total = jnp.dot(w_ref[depth_base + 1], mid_ref[...], preferred_element_type=jnp.float32)
        total = total + jnp.dot(w_ref[depth_base], lo_ref[...], preferred_element_type=jnp.float32)
        total = total + jnp.dot(w_ref[depth_base + 2], up_ref[...], preferred_element_type=jnp.float32)
        h = jnp.maximum(total, 0.0).astype(jnp.bfloat16)
    if plane_bases:
        ok = _masks(h.shape[1])
        for base in plane_bases:
            h = jnp.maximum(_plane(h, w_ref, base, ok), 0.0).astype(jnp.bfloat16)
    o_ref[...] = h


def layer_kernel(inputs, w, depth_base=None, plane_bases=()):
    shape = inputs[0].shape
    return pl.pallas_call(
        functools.partial(_kernel, depth_base=depth_base, plane_bases=tuple(plane_bases)),
        out_shape=jax.ShapeDtypeStruct(shape, jnp.bfloat16),
    )(*inputs, w)


def local(volume, plane_a, plane_b, depth):
    layers, out_part, chans = plane_a.shape[:3]
    part, slab, flat = volume.shape
    parts = lax.axis_size("ch")
    slices = slab // parts
    weights = pack_weights(plane_a, plane_b, depth)
    taps = weights.shape[0]
    half = parts // 2
    flipped = (lax.axis_index("gz") // 2) % 2 == 1
    chunks = swap_halves(volume.reshape(part, parts, slices, flat), 1, flipped)
    sent_volume = jnp.transpose(chunks, (1, 0, 2, 3))
    sent_volume = sent_volume.reshape(parts, part * slices, flat)
    sent_weights = jnp.broadcast_to(
        weights.reshape(1, -1, flat), (parts, taps * out_part * chans // flat, flat)
    )
    sent = jnp.concatenate([sent_volume, sent_weights], axis=1)
    got = lax.all_to_all(sent, "ch", split_axis=0, concat_axis=0, tiled=True)
    got = got.reshape(parts, -1, flat)
    h = got[:, : part * slices].reshape(parts * part, slices * flat)
    w = got[:, part * slices :].reshape(parts, taps, out_part, chans)
    w = jnp.transpose(w, (1, 0, 2, 3)).reshape(taps, parts * out_part, chans)
    nine = 9 * layers

    def bases(layer_index):
        return (layer_index * 9, nine + layer_index * 9)

    second = layer_kernel([h], w, None, bases(0))
    for layer_index in range(layers):
        lower = from_behind(second, 2, half)
        upper = from_behind(second, -2, half)
        following = bases(layer_index + 1) if layer_index + 1 < layers else ()
        second = layer_kernel(
            [lower, second, upper], w, 2 * nine + layer_index * 3, following
        )
    h = second.reshape(parts * part, slices, flat)
    h = lax.all_to_all(h, "ch", split_axis=0, concat_axis=1, tiled=True)
    h = swap_halves(h.reshape(part, parts, slices, flat), 1, flipped)
    return h.reshape(part, slab, flat)


def solution(mesh):
    return jax.shard_map(
        local,
        mesh=mesh,
        in_specs=(
            P("ch", "gz", None),
            P(None, "ch", None, None, None),
            P(None, "ch", None, None, None),
            P(None, "ch", None, None),
        ),
        out_specs=P("ch", "gz", None),
        check_vma=False,
    )
```

```python
import functools

import jax
import jax.numpy as jnp
from jax import lax
from jax.experimental import pallas as pl
from jax.experimental.pallas import tpu as pltpu
from jax.sharding import PartitionSpec as P

X = 64
Y = 8


def from_behind(block, distance, swap):
    slabs, parts = lax.axis_size("gz"), lax.axis_size("ch")
    route = [
        ((g - distance) * parts + (c ^ swap), g * parts + c)
        for g in range(slabs)
        if 0 <= g - distance < slabs
        for c in range(parts)
    ]
    return lax.ppermute(block, ("gz", "ch"), route)


def swap_halves(block, axis, flag):
    shape = block.shape
    halves = block.reshape(shape[:axis] + (2, shape[axis] // 2) + shape[axis + 1 :])
    swapped = jnp.flip(halves, axis)
    return jnp.where(flag, swapped, halves).reshape(shape)


def pack_weights(plane_a, plane_b, depth):
    layers, out_part, chans = plane_a.shape[:3]
    taps_a = jnp.transpose(plane_a, (0, 3, 4, 1, 2)).reshape(-1, out_part, chans)
    taps_b = jnp.transpose(plane_b, (0, 3, 4, 1, 2)).reshape(-1, out_part, chans)
    taps_d = jnp.transpose(depth, (0, 3, 1, 2)).reshape(-1, out_part, chans)
    return jnp.concatenate([taps_a, taps_b, taps_d], axis=0)


def _masks(width):
    p = lax.broadcasted_iota(jnp.int32, (1, width), 1)
    yy = p % Y
    xx = (p // Y) % X
    xm = [xx >= 1, None, xx <= X - 2]
    ym = [yy >= 1, None, yy <= Y - 2]
    ok = []
    for a in range(3):
        row = []
        for b in range(3):
            if xm[a] is None:
                row.append(ym[b])
            elif ym[b] is None:
                row.append(xm[a])
            else:
                row.append(jnp.logical_and(xm[a], ym[b]))
        ok.append(row)
    return ok


def _plane(x, w, ok):
    width = x.shape[1]
    pieces = []
    for a in range(3):
        for b in range(3):
            d = (a - 1) * Y + (b - 1)
            moved = x if d == 0 else pltpu.roll(x, (-d) % width, 1)
            mask = ok[a][b]
            if mask is not None:
                moved = jnp.where(mask, moved, jnp.zeros_like(moved))
            pieces.append(moved)
    stacked = jnp.concatenate(pieces, axis=0)
    return jnp.dot(w, stacked, preferred_element_type=jnp.float32)


def _kernel(*refs, depth_index, plane_indices):
    if depth_index is None:
        x_ref, wp_ref, wd_ref, o_ref = refs
        h = x_ref[...]
    else:
        lo_ref, mid_ref, up_ref, wp_ref, wd_ref, o_ref = refs
        stacked = jnp.concatenate([lo_ref[...], mid_ref[...], up_ref[...]], axis=0)
        total = jnp.dot(wd_ref[depth_index], stacked, preferred_element_type=jnp.float32)
        h = jnp.maximum(total, 0.0).astype(jnp.bfloat16)
    if plane_indices:
        ok = _masks(h.shape[1])
        for index in plane_indices:
            h = jnp.maximum(_plane(h, wp_ref[index], ok), 0.0).astype(jnp.bfloat16)
    o_ref[...] = h


def layer_kernel(inputs, wp, wd, depth_index=None, plane_indices=()):
    shape = inputs[0].shape
    return pl.pallas_call(
        functools.partial(_kernel, depth_index=depth_index, plane_indices=tuple(plane_indices)),
        out_shape=jax.ShapeDtypeStruct(shape, jnp.bfloat16),
    )(*inputs, wp, wd)


def local(volume, plane_a, plane_b, depth):
    layers, out_part, chans = plane_a.shape[:3]
    part, slab, flat = volume.shape
    parts = lax.axis_size("ch")
    slices = slab // parts
    weights = pack_weights(plane_a, plane_b, depth)
    taps = weights.shape[0]
    half = parts // 2
    flipped = (lax.axis_index("gz") // 2) % 2 == 1
    chunks = swap_halves(volume.reshape(part, parts, slices, flat), 1, flipped)
    sent_volume = jnp.transpose(chunks, (1, 0, 2, 3))
    sent_volume = sent_volume.reshape(parts, part * slices, flat)
    sent_weights = jnp.broadcast_to(
        weights.reshape(1, -1, flat), (parts, taps * out_part * chans // flat, flat)
    )
    sent = jnp.concatenate([sent_volume, sent_weights], axis=1)
    got = lax.all_to_all(sent, "ch", split_axis=0, concat_axis=0, tiled=True)
    got = got.reshape(parts, -1, flat)
    h = got[:, : part * slices].reshape(parts * part, slices * flat)
    w = got[:, part * slices :].reshape(parts, taps, out_part, chans)
    nine = 9 * layers
    wp = w[:, : 2 * nine].reshape(parts, 2, layers, 9, out_part, chans)
    wp = jnp.transpose(wp, (2, 1, 0, 4, 3, 5)).reshape(2 * layers, parts * out_part, 9 * chans)
    wd = w[:, 2 * nine :].reshape(parts, layers, 3, out_part, chans)
    wd = jnp.transpose(wd, (1, 0, 3, 2, 4)).reshape(layers, parts * out_part, 3 * chans)

    def convs(layer_index):
        return (2 * layer_index, 2 * layer_index + 1)

    second = layer_kernel([h], wp, wd, None, convs(0))
    for layer_index in range(layers):
        lower = from_behind(second, 2, half)
        upper = from_behind(second, -2, half)
        following = convs(layer_index + 1) if layer_index + 1 < layers else ()
        second = layer_kernel([lower, second, upper], wp, wd, layer_index, following)
    h = second.reshape(parts * part, slices, flat)
    h = lax.all_to_all(h, "ch", split_axis=0, concat_axis=1, tiled=True)
    h = swap_halves(h.reshape(part, parts, slices, flat), 1, flipped)
    return h.reshape(part, slab, flat)


def solution(mesh):
    return jax.shard_map(
        local,
        mesh=mesh,
        in_specs=(
            P("ch", "gz", None),
            P(None, "ch", None, None, None),
            P(None, "ch", None, None, None),
            P(None, "ch", None, None),
        ),
        out_specs=P("ch", "gz", None),
        check_vma=False,
    )
```

```python
import functools

import jax
import jax.numpy as jnp
from jax import lax
from jax.experimental import pallas as pl
from jax.experimental.pallas import tpu as pltpu
from jax.sharding import PartitionSpec as P

X = 64
Y = 8


def from_behind(block, distance, swap):
    slabs, parts = lax.axis_size("gz"), lax.axis_size("ch")
    route = [
        ((g - distance) * parts + (c ^ swap), g * parts + c)
        for g in range(slabs)
        if 0 <= g - distance < slabs
        for c in range(parts)
    ]
    return lax.ppermute(block, ("gz", "ch"), route)


def swap_halves(block, axis, flag):
    shape = block.shape
    halves = block.reshape(shape[:axis] + (2, shape[axis] // 2) + shape[axis + 1 :])
    swapped = jnp.flip(halves, axis)
    return jnp.where(flag, swapped, halves).reshape(shape)


PLANE_COLS = 640
DEPTH_COLS = 256


def pack_weights(plane_a, plane_b, depth):
    layers, out_part, chans = plane_a.shape[:3]
    planes = jnp.stack(
        [
            jnp.transpose(plane_a, (1, 0, 3, 4, 2)).reshape(out_part, layers, 9 * chans),
            jnp.transpose(plane_b, (1, 0, 3, 4, 2)).reshape(out_part, layers, 9 * chans),
        ],
        axis=2,
    )
    planes = jnp.pad(planes, ((0, 0), (0, 0), (0, 0), (0, PLANE_COLS - 9 * chans)))
    depths = jnp.transpose(depth, (1, 0, 3, 2)).reshape(out_part, layers, 3 * chans)
    depths = jnp.pad(depths, ((0, 0), (0, 0), (0, DEPTH_COLS - 3 * chans)))
    return jnp.concatenate(
        [planes.reshape(out_part, -1), depths.reshape(out_part, -1)], axis=1
    )


def _masks(width):
    p = lax.broadcasted_iota(jnp.int32, (1, width), 1)
    yy = p % Y
    xx = (p // Y) % X
    xm = [xx >= 1, None, xx <= X - 2]
    ym = [yy >= 1, None, yy <= Y - 2]
    ok = []
    for a in range(3):
        row = []
        for b in range(3):
            if xm[a] is None:
                row.append(ym[b])
            elif ym[b] is None:
                row.append(xm[a])
            else:
                row.append(jnp.logical_and(xm[a], ym[b]))
        ok.append(row)
    return ok


def _plane(x, w, ok):
    width = x.shape[1]
    pieces = []
    for a in range(3):
        for b in range(3):
            d = (a - 1) * Y + (b - 1)
            moved = x if d == 0 else pltpu.roll(x, (-d) % width, 1)
            mask = ok[a][b]
            if mask is not None:
                moved = jnp.where(mask, moved, jnp.zeros_like(moved))
            pieces.append(moved)
    stacked = jnp.concatenate(pieces, axis=0)
    return jnp.dot(w, stacked, preferred_element_type=jnp.float32)


def _kernel(*refs, width, layers, depth_index, plane_indices):
    if depth_index is None:
        src_ref, o_ref = refs
        h = src_ref[:, :width]
    else:
        lo_ref, mid_ref, up_ref, src_ref, o_ref = refs
        chans = mid_ref.shape[0]
        at = width + 2 * layers * PLANE_COLS + depth_index * DEPTH_COLS
        stacked = jnp.concatenate([lo_ref[...], mid_ref[...], up_ref[...]], axis=0)
        w = src_ref[:, at : at + 3 * chans]
        total = jnp.dot(w, stacked, preferred_element_type=jnp.float32)
        h = jnp.maximum(total, 0.0).astype(jnp.bfloat16)
    if plane_indices:
        ok = _masks(h.shape[1])
        chans = h.shape[0]
        for index in plane_indices:
            at = width + index * PLANE_COLS
            w = src_ref[:, at : at + 9 * chans]
            h = jnp.maximum(_plane(h, w, ok), 0.0).astype(jnp.bfloat16)
    o_ref[...] = h


def layer_kernel(inputs, src, width, layers, depth_index=None, plane_indices=()):
    shape = (src.shape[0], width)
    return pl.pallas_call(
        functools.partial(
            _kernel, width=width, layers=layers, depth_index=depth_index, plane_indices=tuple(plane_indices)
        ),
        out_shape=jax.ShapeDtypeStruct(shape, jnp.bfloat16),
    )(*inputs, src)


def local(volume, plane_a, plane_b, depth):
    layers = plane_a.shape[0]
    part, slab, flat = volume.shape
    parts = lax.axis_size("ch")
    slices = slab // parts
    width = slices * flat
    weights = pack_weights(plane_a, plane_b, depth)
    half = parts // 2
    flipped = (lax.axis_index("gz") // 2) % 2 == 1
    chunks = swap_halves(volume.reshape(part, parts, slices, flat), 1, flipped)
    sent_volume = jnp.transpose(chunks, (1, 0, 2, 3)).reshape(parts, part, width)
    sent_weights = jnp.broadcast_to(weights[None], (parts,) + weights.shape)
    sent = jnp.concatenate([sent_volume, sent_weights], axis=2)
    got = lax.all_to_all(sent, "ch", split_axis=0, concat_axis=0, tiled=True)
    src = got.reshape(parts * part, -1)

    def convs(layer_index):
        return (2 * layer_index, 2 * layer_index + 1)

    second = layer_kernel([], src, width, layers, None, convs(0))
    for layer_index in range(layers):
        lower = from_behind(second, 2, half)
        upper = from_behind(second, -2, half)
        following = convs(layer_index + 1) if layer_index + 1 < layers else ()
        second = layer_kernel([lower, second, upper], src, width, layers, layer_index, following)
    h = lax.all_to_all(second, "ch", split_axis=0, concat_axis=0, tiled=True)
    h = swap_halves(h.reshape(parts, part, slices, flat), 0, flipped)
    return jnp.transpose(h, (1, 0, 2, 3)).reshape(part, slab, flat)


def solution(mesh):
    return jax.shard_map(
        local,
        mesh=mesh,
        in_specs=(
            P("ch", "gz", None),
            P(None, "ch", None, None, None),
            P(None, "ch", None, None, None),
            P(None, "ch", None, None),
        ),
        out_specs=P("ch", "gz", None),
        check_vma=False,
    )
```

```python
import functools

import jax
import jax.numpy as jnp
from jax import lax
from jax.experimental import pallas as pl
from jax.experimental.pallas import tpu as pltpu
from jax.sharding import PartitionSpec as P

X = 64
Y = 8


def from_behind(block, distance, swap):
    slabs, parts = lax.axis_size("gz"), lax.axis_size("ch")
    route = [
        ((g - distance) * parts + (c ^ swap), g * parts + c)
        for g in range(slabs)
        if 0 <= g - distance < slabs
        for c in range(parts)
    ]
    return lax.ppermute(block, ("gz", "ch"), route)


def swap_halves(block, axis, flag):
    shape = block.shape
    halves = block.reshape(shape[:axis] + (2, shape[axis] // 2) + shape[axis + 1 :])
    swapped = jnp.flip(halves, axis)
    return jnp.where(flag, swapped, halves).reshape(shape)


PLANE_COLS = 640
DEPTH_COLS = 256


def pack_weights(plane_a, plane_b, depth):
    layers, out_part, chans = plane_a.shape[:3]
    planes = jnp.stack(
        [
            jnp.transpose(plane_a, (1, 0, 3, 4, 2)).reshape(out_part, layers, 9 * chans),
            jnp.transpose(plane_b, (1, 0, 3, 4, 2)).reshape(out_part, layers, 9 * chans),
        ],
        axis=2,
    )
    planes = jnp.pad(planes, ((0, 0), (0, 0), (0, 0), (0, PLANE_COLS - 9 * chans)))
    depths = jnp.transpose(depth, (1, 0, 3, 2)).reshape(out_part, layers, 3 * chans)
    depths = jnp.pad(depths, ((0, 0), (0, 0), (0, DEPTH_COLS - 3 * chans)))
    return jnp.concatenate(
        [planes.reshape(out_part, -1), depths.reshape(out_part, -1)], axis=1
    )


def _masks(width):
    p = lax.broadcasted_iota(jnp.int32, (1, width), 1)
    yy = p % Y
    xx = (p // Y) % X
    xm = [xx >= 1, None, xx <= X - 2]
    ym = [yy >= 1, None, yy <= Y - 2]
    ok = []
    for a in range(3):
        row = []
        for b in range(3):
            if xm[a] is None:
                row.append(ym[b])
            elif ym[b] is None:
                row.append(xm[a])
            else:
                row.append(jnp.logical_and(xm[a], ym[b]))
        ok.append(row)
    return ok


def _plane(x, w, ok):
    width = x.shape[1]
    pieces = []
    for a in range(3):
        for b in range(3):
            d = (a - 1) * Y + (b - 1)
            moved = x if d == 0 else pltpu.roll(x, (-d) % width, 1)
            mask = ok[a][b]
            if mask is not None:
                moved = jnp.where(mask, moved, jnp.zeros_like(moved))
            pieces.append(moved)
    stacked = jnp.concatenate(pieces, axis=0)
    return jnp.dot(w, stacked, preferred_element_type=jnp.float32)


def _kernel(*refs, depth_index, planes):
    refs = list(refs)
    o_ref = refs.pop()
    if depth_index is None:
        h = refs.pop(0)[...]
    else:
        lo_ref, mid_ref, up_ref, wd_ref = refs[:4]
        refs = refs[4:]
        chans = mid_ref.shape[0]
        stacked = jnp.concatenate([lo_ref[...], mid_ref[...], up_ref[...]], axis=0)
        at = depth_index * DEPTH_COLS
        total = jnp.dot(wd_ref[:, at : at + 3 * chans], stacked, preferred_element_type=jnp.float32)
        h = jnp.maximum(total, 0.0).astype(jnp.bfloat16)
    if planes:
        ok = _masks(h.shape[1])
        chans = h.shape[0]
        for w_ref in refs:
            w = w_ref[:, : 9 * chans]
            h = jnp.maximum(_plane(h, w, ok), 0.0).astype(jnp.bfloat16)
    o_ref[...] = h


def layer_kernel(inputs, src, slices, flat, layers, depth_index=None, plane_indices=()):
    chans = src.shape[0]
    depth_block = 2 * layers * PLANE_COLS // (layers * DEPTH_COLS)
    first_slice = (2 * layers * PLANE_COLS + layers * DEPTH_COLS) // flat
    piece = pl.BlockSpec((chans, flat), lambda z: (0, z))
    specs, args = [], []
    if depth_index is None:
        specs.append(pl.BlockSpec((chans, flat), lambda z: (0, first_slice + z)))
        args.append(src)
    else:
        specs += [piece] * 3 + [pl.BlockSpec((chans, layers * DEPTH_COLS), lambda z: (0, depth_block))]
        args += list(inputs) + [src]
    for k in plane_indices:
        specs.append(pl.BlockSpec((chans, PLANE_COLS), lambda z, k=k: (0, k)))
        args.append(src)
    return pl.pallas_call(
        functools.partial(_kernel, depth_index=depth_index, planes=bool(plane_indices)),
        out_shape=jax.ShapeDtypeStruct((chans, slices * flat), jnp.bfloat16),
        grid=(slices,),
        in_specs=specs,
        out_specs=piece,
    )(*args)


def local(volume, plane_a, plane_b, depth):
    layers = plane_a.shape[0]
    part, slab, flat = volume.shape
    parts = lax.axis_size("ch")
    slices = slab // parts
    width = slices * flat
    weights = pack_weights(plane_a, plane_b, depth)
    half = parts // 2
    flipped = (lax.axis_index("gz") // 2) % 2 == 1
    chunks = swap_halves(volume.reshape(part, parts, slices, flat), 1, flipped)
    sent_volume = jnp.transpose(chunks, (1, 0, 2, 3)).reshape(parts, part, width)
    sent_weights = jnp.broadcast_to(weights[None], (parts,) + weights.shape)
    sent = jnp.concatenate([sent_weights, sent_volume], axis=2)
    got = lax.all_to_all(sent, "ch", split_axis=0, concat_axis=0, tiled=True)
    src = got.reshape(parts * part, -1)

    def convs(layer_index):
        return (2 * layer_index, 2 * layer_index + 1)

    second = layer_kernel([], src, slices, flat, layers, None, convs(0))
    for layer_index in range(layers):
        lower = from_behind(second, 2, half)
        upper = from_behind(second, -2, half)
        following = convs(layer_index + 1) if layer_index + 1 < layers else ()
        second = layer_kernel(
            [lower, second, upper], src, slices, flat, layers, layer_index, following
        )
    h = lax.all_to_all(second, "ch", split_axis=0, concat_axis=0, tiled=True)
    h = swap_halves(h.reshape(parts, part, slices, flat), 0, flipped)
    return jnp.transpose(h, (1, 0, 2, 3)).reshape(part, slab, flat)


def solution(mesh):
    return jax.shard_map(
        local,
        mesh=mesh,
        in_specs=(
            P("ch", "gz", None),
            P(None, "ch", None, None, None),
            P(None, "ch", None, None, None),
            P(None, "ch", None, None),
        ),
        out_specs=P("ch", "gz", None),
        check_vma=False,
    )
```

```python
import functools

import jax
import jax.numpy as jnp
from jax import lax
from jax.experimental import pallas as pl
from jax.experimental.pallas import tpu as pltpu
from jax.sharding import Mesh
from jax.sharding import PartitionSpec as P

X = 64
Y = 8
PLANE_COLS = 640
DEPTH_COLS = 256
LAYER_COLS = 2 * PLANE_COLS + DEPTH_COLS
SLAB = ("z", "yh", "core")
GROUP = ("yh", "ch")


def pack_weights(plane_a, plane_b, depth):
    layers, out_part, chans = plane_a.shape[:3]
    pad = ((0, 0), (0, 0), (0, PLANE_COLS - 9 * chans))
    taps_a = jnp.pad(jnp.transpose(plane_a, (1, 0, 3, 4, 2)).reshape(out_part, layers, -1), pad)
    taps_b = jnp.pad(jnp.transpose(plane_b, (1, 0, 3, 4, 2)).reshape(out_part, layers, -1), pad)
    taps_d = jnp.transpose(depth, (1, 0, 3, 2)).reshape(out_part, layers, 3 * chans)
    taps_d = jnp.pad(taps_d, ((0, 0), (0, 0), (0, DEPTH_COLS - 3 * chans)))
    return jnp.concatenate([taps_a, taps_b, taps_d], axis=2)


def _masks(width):
    p = lax.broadcasted_iota(jnp.int32, (1, width), 1)
    yy = p % Y
    xx = (p // Y) % X
    xm = [xx >= 1, None, xx <= X - 2]
    ym = [yy >= 1, None, yy <= Y - 2]
    ok = []
    for a in range(3):
        row = []
        for b in range(3):
            if xm[a] is None:
                row.append(ym[b])
            elif ym[b] is None:
                row.append(xm[a])
            else:
                row.append(jnp.logical_and(xm[a], ym[b]))
        ok.append(row)
    return ok


def _plane(x, w, ok):
    width = x.shape[1]
    pieces = []
    for a in range(3):
        for b in range(3):
            d = (a - 1) * Y + (b - 1)
            moved = x if d == 0 else pltpu.roll(x, (-d) % width, 1)
            mask = ok[a][b]
            if mask is not None:
                moved = jnp.where(mask, moved, jnp.zeros_like(moved))
            pieces.append(moved)
    stacked = jnp.concatenate(pieces, axis=0)
    return jnp.dot(w, stacked, preferred_element_type=jnp.float32)


def _kernel(*refs, depth_layer, plane_layer, vol_cols, chans, split_out):
    if split_out:
        o_refs = refs[-2:]
        refs = refs[:-2]
    else:
        o_refs = refs[-1:]
        refs = refs[:-1]
    src_ref = refs[-1]
    if depth_layer is None:
        h = jnp.concatenate(
            [src_ref[:chans, :vol_cols], src_ref[chans:, :vol_cols]], axis=1
        )
    else:
        lo_ref, low_ref, high_ref, up_ref = refs[:4]
        low, high = low_ref[...], high_ref[...]
        stacked = jnp.concatenate(
            [
                jnp.concatenate([lo_ref[...], low], axis=1),
                jnp.concatenate([low, high], axis=1),
                jnp.concatenate([high, up_ref[...]], axis=1),
            ],
            axis=0,
        )
        rows = slice(depth_layer * chans, (depth_layer + 1) * chans)
        at = vol_cols + 2 * PLANE_COLS
        total = jnp.dot(src_ref[rows, at : at + 3 * chans], stacked, preferred_element_type=jnp.float32)
        h = jnp.maximum(total, 0.0).astype(jnp.bfloat16)
    if plane_layer is not None:
        ok = _masks(h.shape[1])
        rows = slice(plane_layer * chans, (plane_layer + 1) * chans)
        for k in range(2):
            at = vol_cols + k * PLANE_COLS
            w = src_ref[rows, at : at + 9 * chans]
            h = jnp.maximum(_plane(h, w, ok), 0.0).astype(jnp.bfloat16)
    half = h.shape[1] // 2
    if split_out:
        o_refs[0][...] = h[:, :half]
        o_refs[1][...] = h[:, half:]
    else:
        o_refs[0][...] = jnp.concatenate([h[:, :half], h[:, half:]], axis=0)


def layer_kernel(inputs, src, vol_cols, chans, depth_layer, plane_layer, split_out):
    half = jax.ShapeDtypeStruct((chans, vol_cols), jnp.bfloat16)
    out_shape = (half, half) if split_out else jax.ShapeDtypeStruct((2 * chans, vol_cols), jnp.bfloat16)
    return pl.pallas_call(
        functools.partial(
            _kernel,
            depth_layer=depth_layer,
            plane_layer=plane_layer,
            vol_cols=vol_cols,
            chans=chans,
            split_out=split_out,
        ),
        out_shape=out_shape,
    )(*inputs, src)


def shift_z(block, step):
    size = lax.axis_size("z")
    route = [(i, i + step) for i in range(size) if 0 <= i + step < size]
    return lax.ppermute(block, "z", route)


def local(volume, plane_a, plane_b, depth):
    layers, out_part, chans = plane_a.shape[:3]
    part, slab, flat = volume.shape
    members = lax.axis_size("yh") * lax.axis_size("ch")
    per = slab // members
    vol_cols = per * flat
    sent_volume = jnp.transpose(volume.reshape(part, members, per, flat), (1, 0, 2, 3))
    sent_volume = sent_volume.reshape(members, part, vol_cols)
    weights = pack_weights(plane_a, plane_b, depth)
    mine = lax.dynamic_index_in_dim(weights, lax.axis_index("yh"), 1, keepdims=False)
    sent_weights = jnp.broadcast_to(mine[None], (members,) + mine.shape)
    sent = jnp.concatenate([sent_volume, sent_weights], axis=2)
    got = lax.all_to_all(sent, GROUP, split_axis=0, concat_axis=0, tiled=True)
    src = got.reshape(2 * chans, -1)
    low, high = layer_kernel([], src, vol_cols, chans, None, 0, True)
    for layer_index in range(layers):
        below = shift_z(high, 1)
        above = shift_z(low, -1)
        last = layer_index + 1 == layers
        out = layer_kernel(
            [below, low, high, above],
            src,
            vol_cols,
            chans,
            layer_index,
            None if last else layer_index + 1,
            not last,
        )
        if not last:
            low, high = out
    h = lax.all_to_all(out.reshape(members, part, vol_cols), GROUP, split_axis=0, concat_axis=0, tiled=True)
    h = jnp.transpose(h.reshape(members, part, per, flat), (1, 0, 2, 3))
    return h.reshape(part, slab, flat)


def solution(mesh):
    slabs = mesh.shape["gz"]
    split = Mesh(
        mesh.devices.reshape(slabs // 4, 2, 2, mesh.shape["ch"]), ("z", "yh", "core", "ch")
    )
    return jax.shard_map(
        local,
        mesh=split,
        in_specs=(
            P("ch", SLAB, None),
            P(None, "ch", None, None, None),
            P(None, "ch", None, None, None),
            P(None, "ch", None, None),
        ),
        out_specs=P("ch", SLAB, None),
        check_vma=False,
    )
```

```python
import functools

import jax
import jax.numpy as jnp
from jax import lax
from jax.experimental import pallas as pl
from jax.experimental.pallas import tpu as pltpu
from jax.sharding import Mesh
from jax.sharding import PartitionSpec as P

X = 64
Y = 8
PLANE_COLS = 640
DEPTH_COLS = 256
LAYER_COLS = 2 * PLANE_COLS + DEPTH_COLS
SLAB = ("z", "yh", "core")
GROUP = ("yh", "ch")


def pack_weights(plane_a, plane_b, depth):
    layers, out_part, chans = plane_a.shape[:3]
    pad = ((0, 0), (0, 0), (0, PLANE_COLS - 9 * chans))
    taps_a = jnp.pad(jnp.transpose(plane_a, (1, 0, 3, 4, 2)).reshape(out_part, layers, -1), pad)
    taps_b = jnp.pad(jnp.transpose(plane_b, (1, 0, 3, 4, 2)).reshape(out_part, layers, -1), pad)
    taps_d = jnp.transpose(depth, (1, 0, 3, 2)).reshape(out_part, layers, 3 * chans)
    taps_d = jnp.pad(taps_d, ((0, 0), (0, 0), (0, DEPTH_COLS - 3 * chans)))
    return jnp.concatenate([taps_a, taps_b, taps_d], axis=2)


def _masks(width):
    p = lax.broadcasted_iota(jnp.int32, (1, width), 1)
    yy = p % Y
    xx = (p // Y) % X
    xm = [xx >= 1, None, xx <= X - 2]
    ym = [yy >= 1, None, yy <= Y - 2]
    ok = []
    for a in range(3):
        row = []
        for b in range(3):
            if xm[a] is None:
                row.append(ym[b])
            elif ym[b] is None:
                row.append(xm[a])
            else:
                row.append(jnp.logical_and(xm[a], ym[b]))
        ok.append(row)
    return ok


def _plane(x, w, ok):
    width = x.shape[1]
    pieces = []
    for a in range(3):
        for b in range(3):
            d = (a - 1) * Y + (b - 1)
            moved = x if d == 0 else pltpu.roll(x, (-d) % width, 1)
            mask = ok[a][b]
            if mask is not None:
                moved = jnp.where(mask, moved, jnp.zeros_like(moved))
            pieces.append(moved)
    stacked = jnp.concatenate(pieces, axis=0)
    return jnp.dot(w, stacked, preferred_element_type=jnp.float32)


def _kernel(*refs, depth_layer, plane_layer, vol_cols, chans, split_out):
    if split_out:
        o_refs = refs[-2:]
        refs = refs[:-2]
    else:
        o_refs = refs[-1:]
        refs = refs[:-1]
    src_ref = refs[-1]
    if depth_layer is None:
        h = jnp.concatenate(
            [src_ref[:chans, :vol_cols], src_ref[chans:, :vol_cols]], axis=1
        )
    else:
        lo_ref, low_ref, high_ref, up_ref = refs[:4]
        low, high = low_ref[...], high_ref[...]
        stacked = jnp.concatenate(
            [
                jnp.concatenate([lo_ref[...], low], axis=1),
                jnp.concatenate([low, high], axis=1),
                jnp.concatenate([high, up_ref[...]], axis=1),
            ],
            axis=0,
        )
        rows = slice(depth_layer * chans, (depth_layer + 1) * chans)
        at = vol_cols + 2 * PLANE_COLS
        total = jnp.dot(src_ref[rows, at : at + 3 * chans], stacked, preferred_element_type=jnp.float32)
        h = jnp.maximum(total, 0.0).astype(jnp.bfloat16)
    if plane_layer is not None:
        ok = _masks(h.shape[1])
        rows = slice(plane_layer * chans, (plane_layer + 1) * chans)
        for k in range(2):
            at = vol_cols + k * PLANE_COLS
            w = src_ref[rows, at : at + 9 * chans]
            h = jnp.maximum(_plane(h, w, ok), 0.0).astype(jnp.bfloat16)
    half = h.shape[1] // 2
    if split_out:
        o_refs[0][...] = h[:, :half]
        o_refs[1][...] = h[:, half:]
    else:
        o_refs[0][...] = jnp.concatenate([h[:, :half], h[:, half:]], axis=0)


def layer_kernel(inputs, src, vol_cols, chans, depth_layer, plane_layer, split_out):
    half = jax.ShapeDtypeStruct((chans, vol_cols), jnp.bfloat16)
    out_shape = (half, half) if split_out else jax.ShapeDtypeStruct((2 * chans, vol_cols), jnp.bfloat16)
    return pl.pallas_call(
        functools.partial(
            _kernel,
            depth_layer=depth_layer,
            plane_layer=plane_layer,
            vol_cols=vol_cols,
            chans=chans,
            split_out=split_out,
        ),
        out_shape=out_shape,
    )(*inputs, src)


def _half_kernel(*refs, depth_layer, plane_layer, vol_cols, chans, row_half):
    src_ref, o_ref = refs[-2:]
    if depth_layer is None:
        h = src_ref[row_half * chans : (row_half + 1) * chans, :vol_cols]
    else:
        lo_ref, mid_ref, up_ref = refs[:3]
        stacked = jnp.concatenate([lo_ref[...], mid_ref[...], up_ref[...]], axis=0)
        rows = slice(depth_layer * chans, (depth_layer + 1) * chans)
        at = vol_cols + 2 * PLANE_COLS
        total = jnp.dot(src_ref[rows, at : at + 3 * chans], stacked, preferred_element_type=jnp.float32)
        h = jnp.maximum(total, 0.0).astype(jnp.bfloat16)
    ok = _masks(h.shape[1])
    rows = slice(plane_layer * chans, (plane_layer + 1) * chans)
    for k in range(2):
        at = vol_cols + k * PLANE_COLS
        w = src_ref[rows, at : at + 9 * chans]
        h = jnp.maximum(_plane(h, w, ok), 0.0).astype(jnp.bfloat16)
    o_ref[...] = h


def half_kernel(inputs, src, vol_cols, chans, depth_layer, plane_layer, row_half=0):
    return pl.pallas_call(
        functools.partial(
            _half_kernel,
            depth_layer=depth_layer,
            plane_layer=plane_layer,
            vol_cols=vol_cols,
            chans=chans,
            row_half=row_half,
        ),
        out_shape=jax.ShapeDtypeStruct((chans, vol_cols), jnp.bfloat16),
    )(*inputs, src)


def shift_z(block, step):
    size = lax.axis_size("z")
    route = [(i, i + step) for i in range(size) if 0 <= i + step < size]
    return lax.ppermute(block, "z", route)


def local(volume, plane_a, plane_b, depth):
    layers, out_part, chans = plane_a.shape[:3]
    part, slab, flat = volume.shape
    members = lax.axis_size("yh") * lax.axis_size("ch")
    per = slab // members
    vol_cols = per * flat
    sent_volume = jnp.transpose(volume.reshape(part, members, per, flat), (1, 0, 2, 3))
    sent_volume = sent_volume.reshape(members, part, vol_cols)
    weights = pack_weights(plane_a, plane_b, depth)
    mine = lax.dynamic_index_in_dim(weights, lax.axis_index("yh"), 1, keepdims=False)
    sent_weights = jnp.broadcast_to(mine[None], (members,) + mine.shape)
    sent = jnp.concatenate([sent_volume, sent_weights], axis=2)
    got = lax.all_to_all(sent, GROUP, split_axis=0, concat_axis=0, tiled=True)
    src = got.reshape(2 * chans, -1)
    high = half_kernel([], src, vol_cols, chans, None, 0, 1)
    below = shift_z(high, 1)
    low = half_kernel([], src, vol_cols, chans, None, 0, 0)
    above = shift_z(low, -1)
    for layer_index in range(layers - 1):
        new_low = half_kernel([below, low, high], src, vol_cols, chans, layer_index, layer_index + 1)
        new_high = half_kernel([low, high, above], src, vol_cols, chans, layer_index, layer_index + 1)
        low, high = new_low, new_high
        below = shift_z(high, 1)
        above = shift_z(low, -1)
    out = layer_kernel(
        [below, low, high, above], src, vol_cols, chans, layers - 1, None, False
    )
    h = lax.all_to_all(out.reshape(members, part, vol_cols), GROUP, split_axis=0, concat_axis=0, tiled=True)
    h = jnp.transpose(h.reshape(members, part, per, flat), (1, 0, 2, 3))
    return h.reshape(part, slab, flat)


def solution(mesh):
    slabs = mesh.shape["gz"]
    split = Mesh(
        mesh.devices.reshape(slabs // 4, 2, 2, mesh.shape["ch"]), ("z", "yh", "core", "ch")
    )
    return jax.shard_map(
        local,
        mesh=split,
        in_specs=(
            P("ch", SLAB, None),
            P(None, "ch", None, None, None),
            P(None, "ch", None, None, None),
            P(None, "ch", None, None),
        ),
        out_specs=P("ch", SLAB, None),
        check_vma=False,
    )
```

```python
import functools

import jax
import jax.numpy as jnp
from jax import lax
from jax.experimental import pallas as pl
from jax.experimental.pallas import tpu as pltpu
from jax.sharding import Mesh
from jax.sharding import PartitionSpec as P

X = 64
Y = 8
PLANE_COLS = 640
DEPTH_COLS = 256
LAYER_COLS = 2 * PLANE_COLS + DEPTH_COLS
SLAB = ("z", "yh", "core")
GROUP = ("yh", "ch")


def pack_weights(plane_a, plane_b, depth):
    layers, out_part, chans = plane_a.shape[:3]
    pad = ((0, 0), (0, 0), (0, PLANE_COLS - 9 * chans))
    taps_a = jnp.pad(jnp.transpose(plane_a, (1, 0, 3, 4, 2)).reshape(out_part, layers, -1), pad)
    taps_b = jnp.pad(jnp.transpose(plane_b, (1, 0, 3, 4, 2)).reshape(out_part, layers, -1), pad)
    taps_d = jnp.transpose(depth, (1, 0, 3, 2)).reshape(out_part, layers, 3 * chans)
    taps_d = jnp.pad(taps_d, ((0, 0), (0, 0), (0, DEPTH_COLS - 3 * chans)))
    return jnp.concatenate([taps_a, taps_b, taps_d], axis=2)


def _masks(width):
    p = lax.broadcasted_iota(jnp.int32, (1, width), 1)
    yy = p % Y
    xx = (p // Y) % X
    xm = [xx >= 1, None, xx <= X - 2]
    ym = [yy >= 1, None, yy <= Y - 2]
    ok = []
    for a in range(3):
        row = []
        for b in range(3):
            if xm[a] is None:
                row.append(ym[b])
            elif ym[b] is None:
                row.append(xm[a])
            else:
                row.append(jnp.logical_and(xm[a], ym[b]))
        ok.append(row)
    return ok


def _plane(x, w, ok):
    width = x.shape[1]
    pieces = []
    for a in range(3):
        for b in range(3):
            d = (a - 1) * Y + (b - 1)
            moved = x if d == 0 else pltpu.roll(x, (-d) % width, 1)
            mask = ok[a][b]
            if mask is not None:
                moved = jnp.where(mask, moved, jnp.zeros_like(moved))
            pieces.append(moved)
    stacked = jnp.concatenate(pieces, axis=0)
    return jnp.dot(w, stacked, preferred_element_type=jnp.float32)


W_COLS = 2 * PLANE_COLS + DEPTH_COLS
PIECE = 512


def _kernel(*refs, depth, planes, stack_out):
    refs = list(refs)
    o_ref = refs.pop()
    if planes:
        wp_ref = refs.pop()
    if depth:
        wd_ref = refs.pop()
        if len(refs) == 4:
            lo_ref, low_ref, high_ref, up_ref = refs
            low, high = low_ref[...], high_ref[...]
            parts = [
                jnp.concatenate([lo_ref[...], low], axis=1),
                jnp.concatenate([low, high], axis=1),
                jnp.concatenate([high, up_ref[...]], axis=1),
            ]
        else:
            parts = [r[...] for r in refs]
        chans = parts[0].shape[0]
        stacked = jnp.concatenate(parts, axis=0)
        total = jnp.dot(wd_ref[:, : 3 * chans], stacked, preferred_element_type=jnp.float32)
        h = jnp.maximum(total, 0.0).astype(jnp.bfloat16)
    else:
        h = jnp.concatenate([r[...] for r in refs], axis=1)
    if planes:
        ok = _masks(h.shape[1])
        chans = h.shape[0]
        for k in range(2):
            w = wp_ref[:, k * PLANE_COLS : k * PLANE_COLS + 9 * chans]
            h = jnp.maximum(_plane(h, w, ok), 0.0).astype(jnp.bfloat16)
    if stack_out:
        half = h.shape[1] // 2
        o_ref[...] = jnp.concatenate([h[:, :half], h[:, half:]], axis=0)
    else:
        o_ref[...] = h


def layer_kernel(inputs, src, vol_cols, chans, depth_layer=None, plane_layer=None, row_half=0, stack_out=False):
    specs, args = [], []
    if depth_layer is None:
        for j in range(vol_cols // PIECE):
            specs.append(pl.BlockSpec((chans, PIECE), lambda i, j=j: (row_half, W_COLS // PIECE + j)))
            args.append(src)
        width = vol_cols
    else:
        specs += [pl.BlockSpec(inp.shape, lambda i: (0, 0)) for inp in inputs]
        args += list(inputs)
        width = inputs[1].shape[1] * (2 if len(inputs) == 4 else 1)
        specs.append(
            pl.BlockSpec((chans, DEPTH_COLS), lambda i: (depth_layer, 2 * PLANE_COLS // DEPTH_COLS))
        )
        args.append(src)
    if plane_layer is not None:
        specs.append(pl.BlockSpec((chans, 2 * PLANE_COLS), lambda i: (plane_layer, 0)))
        args.append(src)
    if stack_out:
        out_shape = jax.ShapeDtypeStruct((2 * chans, width // 2), jnp.bfloat16)
    else:
        out_shape = jax.ShapeDtypeStruct((chans, width), jnp.bfloat16)
    return pl.pallas_call(
        functools.partial(
            _kernel,
            depth=depth_layer is not None,
            planes=plane_layer is not None,
            stack_out=stack_out,
        ),
        out_shape=out_shape,
        in_specs=specs,
        out_specs=pl.BlockSpec(out_shape.shape, lambda i: (0, 0)),
        grid=(1,),
    )(*args)


def shift_z(block, step):
    size = lax.axis_size("z")
    route = [(i, i + step) for i in range(size) if 0 <= i + step < size]
    return lax.ppermute(block, "z", route)


def local(volume, plane_a, plane_b, depth):
    layers, out_part, chans = plane_a.shape[:3]
    part, slab, flat = volume.shape
    members = lax.axis_size("yh") * lax.axis_size("ch")
    per = slab // members
    vol_cols = per * flat
    sent_volume = jnp.transpose(volume.reshape(part, members, per, flat), (1, 0, 2, 3))
    sent_volume = sent_volume.reshape(members, part, vol_cols)
    weights = pack_weights(plane_a, plane_b, depth)
    mine = lax.dynamic_index_in_dim(weights, lax.axis_index("yh"), 1, keepdims=False)
    sent_weights = jnp.broadcast_to(mine[None], (members,) + mine.shape)
    sent = jnp.concatenate([sent_weights, sent_volume], axis=2)
    got = lax.all_to_all(sent, GROUP, split_axis=0, concat_axis=0, tiled=True)
    src = got.reshape(2 * chans, -1)
    high = layer_kernel([], src, vol_cols, chans, None, 0, 1)
    below = shift_z(high, 1)
    low = layer_kernel([], src, vol_cols, chans, None, 0, 0)
    above = shift_z(low, -1)
    for layer_index in range(layers - 1):
        new_low = layer_kernel([below, low, high], src, vol_cols, chans, layer_index, layer_index + 1)
        new_high = layer_kernel([low, high, above], src, vol_cols, chans, layer_index, layer_index + 1)
        low, high = new_low, new_high
        below = shift_z(high, 1)
        above = shift_z(low, -1)
    out = layer_kernel(
        [below, low, high, above], src, vol_cols, chans, layers - 1, None, stack_out=True
    )
    h = lax.all_to_all(out.reshape(members, part, vol_cols), GROUP, split_axis=0, concat_axis=0, tiled=True)
    h = jnp.transpose(h.reshape(members, part, per, flat), (1, 0, 2, 3))
    return h.reshape(part, slab, flat)


def solution(mesh):
    slabs = mesh.shape["gz"]
    split = Mesh(
        mesh.devices.reshape(slabs // 4, 2, 2, mesh.shape["ch"]), ("z", "yh", "core", "ch")
    )
    return jax.shard_map(
        local,
        mesh=split,
        in_specs=(
            P("ch", SLAB, None),
            P(None, "ch", None, None, None),
            P(None, "ch", None, None, None),
            P(None, "ch", None, None),
        ),
        out_specs=P("ch", SLAB, None),
        check_vma=False,
    )
```

```python
import functools

import jax
import jax.numpy as jnp
from jax import lax
from jax.experimental import pallas as pl
from jax.experimental.pallas import tpu as pltpu
from jax.sharding import Mesh
from jax.sharding import PartitionSpec as P

X = 64
Y = 8
PLANE_COLS = 640
DEPTH_COLS = 256
LAYER_COLS = 2 * PLANE_COLS + DEPTH_COLS
SLAB = ("z", "yh", "core")
GROUP = ("yh", "ch")


ANYWHERE_VMEM = pl.BlockSpec(memory_space=pltpu.VMEM)


def in_vmem(arrays):
    return [pltpu.with_memory_space_constraint(a, pltpu.VMEM) for a in arrays]


def pack_weights(plane_a, plane_b, depth):
    layers, out_part, chans = plane_a.shape[:3]
    pad = ((0, 0), (0, 0), (0, PLANE_COLS - 9 * chans))
    taps_a = jnp.pad(jnp.transpose(plane_a, (1, 0, 3, 4, 2)).reshape(out_part, layers, -1), pad)
    taps_b = jnp.pad(jnp.transpose(plane_b, (1, 0, 3, 4, 2)).reshape(out_part, layers, -1), pad)
    taps_d = jnp.transpose(depth, (1, 0, 3, 2)).reshape(out_part, layers, 3 * chans)
    taps_d = jnp.pad(taps_d, ((0, 0), (0, 0), (0, DEPTH_COLS - 3 * chans)))
    return jnp.concatenate([taps_a, taps_b, taps_d], axis=2)


def _masks(width):
    p = lax.broadcasted_iota(jnp.int32, (1, width), 1)
    yy = p % Y
    xx = (p // Y) % X
    xm = [xx >= 1, None, xx <= X - 2]
    ym = [yy >= 1, None, yy <= Y - 2]
    ok = []
    for a in range(3):
        row = []
        for b in range(3):
            if xm[a] is None:
                row.append(ym[b])
            elif ym[b] is None:
                row.append(xm[a])
            else:
                row.append(jnp.logical_and(xm[a], ym[b]))
        ok.append(row)
    return ok


def _plane(x, w, ok):
    width = x.shape[1]
    pieces = []
    for a in range(3):
        for b in range(3):
            d = (a - 1) * Y + (b - 1)
            moved = x if d == 0 else pltpu.roll(x, (-d) % width, 1)
            mask = ok[a][b]
            if mask is not None:
                moved = jnp.where(mask, moved, jnp.zeros_like(moved))
            pieces.append(moved)
    stacked = jnp.concatenate(pieces, axis=0)
    return jnp.dot(w, stacked, preferred_element_type=jnp.float32)


def _kernel(*refs, depth_layer, plane_layer, vol_cols, chans, split_out):
    if split_out:
        o_refs = refs[-2:]
        refs = refs[:-2]
    else:
        o_refs = refs[-1:]
        refs = refs[:-1]
    src_ref = refs[-1]
    if depth_layer is None:
        h = jnp.concatenate(
            [src_ref[:chans, :vol_cols], src_ref[chans:, :vol_cols]], axis=1
        )
    else:
        lo_ref, low_ref, high_ref, up_ref = refs[:4]
        low, high = low_ref[...], high_ref[...]
        stacked = jnp.concatenate(
            [
                jnp.concatenate([lo_ref[...], low], axis=1),
                jnp.concatenate([low, high], axis=1),
                jnp.concatenate([high, up_ref[...]], axis=1),
            ],
            axis=0,
        )
        rows = slice(depth_layer * chans, (depth_layer + 1) * chans)
        at = vol_cols + 2 * PLANE_COLS
        total = jnp.dot(src_ref[rows, at : at + 3 * chans], stacked, preferred_element_type=jnp.float32)
        h = jnp.maximum(total, 0.0).astype(jnp.bfloat16)
    if plane_layer is not None:
        ok = _masks(h.shape[1])
        rows = slice(plane_layer * chans, (plane_layer + 1) * chans)
        for k in range(2):
            at = vol_cols + k * PLANE_COLS
            w = src_ref[rows, at : at + 9 * chans]
            h = jnp.maximum(_plane(h, w, ok), 0.0).astype(jnp.bfloat16)
    half = h.shape[1] // 2
    if split_out:
        o_refs[0][...] = h[:, :half]
        o_refs[1][...] = h[:, half:]
    else:
        o_refs[0][...] = jnp.concatenate([h[:, :half], h[:, half:]], axis=0)


def layer_kernel(inputs, src, vol_cols, chans, depth_layer, plane_layer, split_out):
    half = jax.ShapeDtypeStruct((chans, vol_cols), jnp.bfloat16)
    out_shape = (half, half) if split_out else jax.ShapeDtypeStruct((2 * chans, vol_cols), jnp.bfloat16)
    return pl.pallas_call(
        functools.partial(
            _kernel,
            depth_layer=depth_layer,
            plane_layer=plane_layer,
            vol_cols=vol_cols,
            chans=chans,
            split_out=split_out,
        ),
        out_shape=out_shape,
        in_specs=[ANYWHERE_VMEM] * (len(inputs) + 1),
        out_specs=(ANYWHERE_VMEM, ANYWHERE_VMEM) if split_out else ANYWHERE_VMEM,
    )(*in_vmem(list(inputs) + [src]))


def _half_kernel(*refs, depth_layer, plane_layer, vol_cols, chans, row_half):
    src_ref, o_ref = refs[-2:]
    if depth_layer is None:
        h = src_ref[row_half * chans : (row_half + 1) * chans, :vol_cols]
    else:
        lo_ref, mid_ref, up_ref = refs[:3]
        stacked = jnp.concatenate([lo_ref[...], mid_ref[...], up_ref[...]], axis=0)
        rows = slice(depth_layer * chans, (depth_layer + 1) * chans)
        at = vol_cols + 2 * PLANE_COLS
        total = jnp.dot(src_ref[rows, at : at + 3 * chans], stacked, preferred_element_type=jnp.float32)
        h = jnp.maximum(total, 0.0).astype(jnp.bfloat16)
    ok = _masks(h.shape[1])
    rows = slice(plane_layer * chans, (plane_layer + 1) * chans)
    for k in range(2):
        at = vol_cols + k * PLANE_COLS
        w = src_ref[rows, at : at + 9 * chans]
        h = jnp.maximum(_plane(h, w, ok), 0.0).astype(jnp.bfloat16)
    o_ref[...] = h


def half_kernel(inputs, src, vol_cols, chans, depth_layer, plane_layer, row_half=0):
    return pl.pallas_call(
        functools.partial(
            _half_kernel,
            depth_layer=depth_layer,
            plane_layer=plane_layer,
            vol_cols=vol_cols,
            chans=chans,
            row_half=row_half,
        ),
        out_shape=jax.ShapeDtypeStruct((chans, vol_cols), jnp.bfloat16),
        in_specs=[ANYWHERE_VMEM] * (len(inputs) + 1),
        out_specs=ANYWHERE_VMEM,
    )(*in_vmem(list(inputs) + [src]))


def shift_z(block, step):
    size = lax.axis_size("z")
    route = [(i, i + step) for i in range(size) if 0 <= i + step < size]
    return lax.ppermute(block, "z", route)


def local(volume, plane_a, plane_b, depth):
    layers, out_part, chans = plane_a.shape[:3]
    part, slab, flat = volume.shape
    members = lax.axis_size("yh") * lax.axis_size("ch")
    per = slab // members
    vol_cols = per * flat
    sent_volume = jnp.transpose(volume.reshape(part, members, per, flat), (1, 0, 2, 3))
    sent_volume = sent_volume.reshape(members, part, vol_cols)
    weights = pack_weights(plane_a, plane_b, depth)
    mine = lax.dynamic_index_in_dim(weights, lax.axis_index("yh"), 1, keepdims=False)
    sent_weights = jnp.broadcast_to(mine[None], (members,) + mine.shape)
    sent = jnp.concatenate([sent_volume, sent_weights], axis=2)
    got = lax.all_to_all(sent, GROUP, split_axis=0, concat_axis=0, tiled=True)
    src = got.reshape(2 * chans, -1)
    high = half_kernel([], src, vol_cols, chans, None, 0, 1)
    below = shift_z(high, 1)
    low = half_kernel([], src, vol_cols, chans, None, 0, 0)
    above = shift_z(low, -1)
    for layer_index in range(layers - 1):
        new_low = half_kernel([below, low, high], src, vol_cols, chans, layer_index, layer_index + 1)
        new_high = half_kernel([low, high, above], src, vol_cols, chans, layer_index, layer_index + 1)
        low, high = new_low, new_high
        below = shift_z(high, 1)
        above = shift_z(low, -1)
    out = layer_kernel(
        [below, low, high, above], src, vol_cols, chans, layers - 1, None, False
    )
    h = lax.all_to_all(out.reshape(members, part, vol_cols), GROUP, split_axis=0, concat_axis=0, tiled=True)
    h = jnp.transpose(h.reshape(members, part, per, flat), (1, 0, 2, 3))
    return h.reshape(part, slab, flat)


def solution(mesh):
    slabs = mesh.shape["gz"]
    split = Mesh(
        mesh.devices.reshape(slabs // 4, 2, 2, mesh.shape["ch"]), ("z", "yh", "core", "ch")
    )
    return jax.shard_map(
        local,
        mesh=split,
        in_specs=(
            P("ch", SLAB, None),
            P(None, "ch", None, None, None),
            P(None, "ch", None, None, None),
            P(None, "ch", None, None),
        ),
        out_specs=P("ch", SLAB, None),
        check_vma=False,
    )
```

```python
import functools

import jax
import jax.numpy as jnp
from jax import lax
from jax.experimental import pallas as pl
from jax.experimental.pallas import tpu as pltpu
from jax.sharding import Mesh
from jax.sharding import PartitionSpec as P

X = 64
Y = 8
PLANE_COLS = 640
DEPTH_COLS = 256
LAYER_COLS = 2 * PLANE_COLS + DEPTH_COLS
SLAB = ("z", "yh", "core")
GROUP = ("yh", "ch")


ANYWHERE_VMEM = pl.BlockSpec(memory_space=pltpu.VMEM)


def in_vmem(arrays):
    return [pltpu.with_memory_space_constraint(a, pltpu.VMEM) for a in arrays]


def pack_weights(plane_a, plane_b, depth):
    layers, out_part, chans = plane_a.shape[:3]
    pad = ((0, 0), (0, 0), (0, PLANE_COLS - 9 * chans))
    taps_a = jnp.pad(jnp.transpose(plane_a, (1, 0, 3, 4, 2)).reshape(out_part, layers, -1), pad)
    taps_b = jnp.pad(jnp.transpose(plane_b, (1, 0, 3, 4, 2)).reshape(out_part, layers, -1), pad)
    taps_d = jnp.transpose(depth, (1, 0, 3, 2)).reshape(out_part, layers, 3 * chans)
    taps_d = jnp.pad(taps_d, ((0, 0), (0, 0), (0, DEPTH_COLS - 3 * chans)))
    return jnp.concatenate([taps_a, taps_b, taps_d], axis=2)


def _masks(width):
    p = lax.broadcasted_iota(jnp.int32, (1, width), 1)
    yy = p % Y
    xx = (p // Y) % X
    xm = [xx >= 1, None, xx <= X - 2]
    ym = [yy >= 1, None, yy <= Y - 2]
    ok = []
    for a in range(3):
        row = []
        for b in range(3):
            if xm[a] is None:
                row.append(ym[b])
            elif ym[b] is None:
                row.append(xm[a])
            else:
                row.append(jnp.logical_and(xm[a], ym[b]))
        ok.append(row)
    return ok


def _plane(x, w, ok):
    width = x.shape[1]
    pieces = []
    for a in range(3):
        for b in range(3):
            d = (a - 1) * Y + (b - 1)
            moved = x if d == 0 else pltpu.roll(x, (-d) % width, 1)
            mask = ok[a][b]
            if mask is not None:
                moved = jnp.where(mask, moved, jnp.zeros_like(moved))
            pieces.append(moved)
    stacked = jnp.concatenate(pieces, axis=0)
    return jnp.dot(w, stacked, preferred_element_type=jnp.float32)


def _kernel(*refs, depth_layer, plane_layer, vol_cols, chans, split_out):
    if split_out:
        o_refs = refs[-2:]
        refs = refs[:-2]
    else:
        o_refs = refs[-1:]
        refs = refs[:-1]
    src_ref = refs[-1]
    if depth_layer is None:
        h = jnp.concatenate(
            [src_ref[:chans, :vol_cols], src_ref[chans:, :vol_cols]], axis=1
        )
    else:
        lo_ref, low_ref, high_ref, up_ref = refs[:4]
        low, high = low_ref[...], high_ref[...]
        stacked = jnp.concatenate(
            [
                jnp.concatenate([lo_ref[...], low], axis=1),
                jnp.concatenate([low, high], axis=1),
                jnp.concatenate([high, up_ref[...]], axis=1),
            ],
            axis=0,
        )
        rows = slice(depth_layer * chans, (depth_layer + 1) * chans)
        at = vol_cols + 2 * PLANE_COLS
        total = jnp.dot(src_ref[rows, at : at + 3 * chans], stacked, preferred_element_type=jnp.float32)
        h = jnp.maximum(total, 0.0).astype(jnp.bfloat16)
    if plane_layer is not None:
        ok = _masks(h.shape[1])
        rows = slice(plane_layer * chans, (plane_layer + 1) * chans)
        for k in range(2):
            at = vol_cols + k * PLANE_COLS
            w = src_ref[rows, at : at + 9 * chans]
            h = jnp.maximum(_plane(h, w, ok), 0.0).astype(jnp.bfloat16)
    half = h.shape[1] // 2
    if split_out:
        o_refs[0][...] = h[:, :half]
        o_refs[1][...] = h[:, half:]
    else:
        o_refs[0][...] = jnp.concatenate([h[:, :half], h[:, half:]], axis=0)


def layer_kernel(inputs, src, vol_cols, chans, depth_layer, plane_layer, split_out):
    half = pltpu.VMEM((chans, vol_cols), jnp.bfloat16)
    out_shape = (half, half) if split_out else pltpu.VMEM((2 * chans, vol_cols), jnp.bfloat16)
    return pl.pallas_call(
        functools.partial(
            _kernel,
            depth_layer=depth_layer,
            plane_layer=plane_layer,
            vol_cols=vol_cols,
            chans=chans,
            split_out=split_out,
        ),
        out_shape=out_shape,
        in_specs=[ANYWHERE_VMEM] * (len(inputs) + 1),
        out_specs=(ANYWHERE_VMEM, ANYWHERE_VMEM) if split_out else ANYWHERE_VMEM,
    )(*in_vmem(list(inputs) + [src]))


def _half_kernel(*refs, depth_layer, plane_layer, vol_cols, chans, row_half):
    src_ref, o_ref = refs[-2:]
    if depth_layer is None:
        h = src_ref[row_half * chans : (row_half + 1) * chans, :vol_cols]
    else:
        lo_ref, mid_ref, up_ref = refs[:3]
        stacked = jnp.concatenate([lo_ref[...], mid_ref[...], up_ref[...]], axis=0)
        rows = slice(depth_layer * chans, (depth_layer + 1) * chans)
        at = vol_cols + 2 * PLANE_COLS
        total = jnp.dot(src_ref[rows, at : at + 3 * chans], stacked, preferred_element_type=jnp.float32)
        h = jnp.maximum(total, 0.0).astype(jnp.bfloat16)
    ok = _masks(h.shape[1])
    rows = slice(plane_layer * chans, (plane_layer + 1) * chans)
    for k in range(2):
        at = vol_cols + k * PLANE_COLS
        w = src_ref[rows, at : at + 9 * chans]
        h = jnp.maximum(_plane(h, w, ok), 0.0).astype(jnp.bfloat16)
    o_ref[...] = h


def half_kernel(inputs, src, vol_cols, chans, depth_layer, plane_layer, row_half=0):
    return pl.pallas_call(
        functools.partial(
            _half_kernel,
            depth_layer=depth_layer,
            plane_layer=plane_layer,
            vol_cols=vol_cols,
            chans=chans,
            row_half=row_half,
        ),
        out_shape=pltpu.VMEM((chans, vol_cols), jnp.bfloat16),
        in_specs=[ANYWHERE_VMEM] * (len(inputs) + 1),
        out_specs=ANYWHERE_VMEM,
    )(*in_vmem(list(inputs) + [src]))


def shift_z(block, step):
    size = lax.axis_size("z")
    route = [(i, i + step) for i in range(size) if 0 <= i + step < size]
    return lax.ppermute(block, "z", route)


def local(volume, plane_a, plane_b, depth):
    layers, out_part, chans = plane_a.shape[:3]
    part, slab, flat = volume.shape
    members = lax.axis_size("yh") * lax.axis_size("ch")
    per = slab // members
    vol_cols = per * flat
    sent_volume = jnp.transpose(volume.reshape(part, members, per, flat), (1, 0, 2, 3))
    sent_volume = sent_volume.reshape(members, part, vol_cols)
    weights = pack_weights(plane_a, plane_b, depth)
    mine = lax.dynamic_index_in_dim(weights, lax.axis_index("yh"), 1, keepdims=False)
    sent_weights = jnp.broadcast_to(mine[None], (members,) + mine.shape)
    sent = jnp.concatenate([sent_volume, sent_weights], axis=2)
    got = lax.all_to_all(sent, GROUP, split_axis=0, concat_axis=0, tiled=True)
    src = got.reshape(2 * chans, -1)
    high = half_kernel([], src, vol_cols, chans, None, 0, 1)
    below = shift_z(high, 1)
    low = half_kernel([], src, vol_cols, chans, None, 0, 0)
    above = shift_z(low, -1)
    for layer_index in range(layers - 1):
        new_low = half_kernel([below, low, high], src, vol_cols, chans, layer_index, layer_index + 1)
        new_high = half_kernel([low, high, above], src, vol_cols, chans, layer_index, layer_index + 1)
        low, high = new_low, new_high
        below = shift_z(high, 1)
        above = shift_z(low, -1)
    out = layer_kernel(
        [below, low, high, above], src, vol_cols, chans, layers - 1, None, False
    )
    h = lax.all_to_all(out.reshape(members, part, vol_cols), GROUP, split_axis=0, concat_axis=0, tiled=True)
    h = jnp.transpose(h.reshape(members, part, per, flat), (1, 0, 2, 3))
    return h.reshape(part, slab, flat)


def solution(mesh):
    slabs = mesh.shape["gz"]
    split = Mesh(
        mesh.devices.reshape(slabs // 4, 2, 2, mesh.shape["ch"]), ("z", "yh", "core", "ch")
    )
    return jax.shard_map(
        local,
        mesh=split,
        in_specs=(
            P("ch", SLAB, None),
            P(None, "ch", None, None, None),
            P(None, "ch", None, None, None),
            P(None, "ch", None, None),
        ),
        out_specs=P("ch", SLAB, None),
        check_vma=False,
    )
```

```python
import functools

import jax
import jax.numpy as jnp
from jax import lax
from jax.experimental import pallas as pl
from jax.experimental.pallas import tpu as pltpu
from jax.sharding import Mesh
from jax.sharding import PartitionSpec as P

X = 64
Y = 8
SLAB = ("z", "yh", "core")
GROUP = ("yh", "ch")


ANYWHERE_VMEM = pl.BlockSpec(memory_space=pltpu.VMEM)


def in_vmem(arrays):
    return [pltpu.with_memory_space_constraint(a, pltpu.VMEM) for a in arrays]


def pack_weights(plane_a, plane_b, depth):
    layers, out_part, chans = plane_a.shape[:3]
    planes = jnp.transpose(jnp.stack([plane_a, plane_b]), (2, 1, 0, 4, 5, 3))
    planes = planes.reshape(out_part, layers, 18 * chans)
    taps_d = jnp.transpose(depth, (1, 0, 3, 2)).reshape(out_part, layers, 3 * chans)
    return jnp.concatenate([planes, taps_d], axis=2)


def _masks(width):
    p = lax.broadcasted_iota(jnp.int32, (1, width), 1)
    yy = p % Y
    xx = (p // Y) % X
    xm = [xx >= 1, None, xx <= X - 2]
    ym = [yy >= 1, None, yy <= Y - 2]
    ok = []
    for a in range(3):
        row = []
        for b in range(3):
            if xm[a] is None:
                row.append(ym[b])
            elif ym[b] is None:
                row.append(xm[a])
            else:
                row.append(jnp.logical_and(xm[a], ym[b]))
        ok.append(row)
    return ok


def _plane(x, w, ok):
    width = x.shape[1]
    pieces = []
    for a in range(3):
        for b in range(3):
            d = (a - 1) * Y + (b - 1)
            moved = x if d == 0 else pltpu.roll(x, (-d) % width, 1)
            mask = ok[a][b]
            if mask is not None:
                moved = jnp.where(mask, moved, jnp.zeros_like(moved))
            pieces.append(moved)
    stacked = jnp.concatenate(pieces, axis=0)
    return jnp.dot(w, stacked, preferred_element_type=jnp.float32)


def _kernel(*refs, depth_layer, plane_layer, vol_cols, chans, split_out):
    if split_out:
        o_refs = refs[-2:]
        refs = refs[:-2]
    else:
        o_refs = refs[-1:]
        refs = refs[:-1]
    src_ref = refs[-1]
    if depth_layer is None:
        h = jnp.concatenate(
            [src_ref[:chans, :vol_cols], src_ref[chans:, :vol_cols]], axis=1
        )
    else:
        lo_ref, low_ref, high_ref, up_ref = refs[:4]
        low, high = low_ref[...], high_ref[...]
        stacked = jnp.concatenate(
            [
                jnp.concatenate([lo_ref[...], low], axis=1),
                jnp.concatenate([low, high], axis=1),
                jnp.concatenate([high, up_ref[...]], axis=1),
            ],
            axis=0,
        )
        rows = slice(depth_layer * chans, (depth_layer + 1) * chans)
        at = vol_cols + 18 * chans
        total = jnp.dot(src_ref[rows, at : at + 3 * chans], stacked, preferred_element_type=jnp.float32)
        h = jnp.maximum(total, 0.0).astype(jnp.bfloat16)
    if plane_layer is not None:
        ok = _masks(h.shape[1])
        rows = slice(plane_layer * chans, (plane_layer + 1) * chans)
        for k in range(2):
            at = vol_cols + k * 9 * chans
            w = src_ref[rows, at : at + 9 * chans]
            h = jnp.maximum(_plane(h, w, ok), 0.0).astype(jnp.bfloat16)
    half = h.shape[1] // 2
    if split_out:
        o_refs[0][...] = h[:, :half]
        o_refs[1][...] = h[:, half:]
    else:
        o_refs[0][...] = jnp.concatenate([h[:, :half], h[:, half:]], axis=0)


def layer_kernel(inputs, src, vol_cols, chans, depth_layer, plane_layer, split_out):
    half = pltpu.VMEM((chans, vol_cols), jnp.bfloat16)
    out_shape = (half, half) if split_out else pltpu.VMEM((2 * chans, vol_cols), jnp.bfloat16)
    return pl.pallas_call(
        functools.partial(
            _kernel,
            depth_layer=depth_layer,
            plane_layer=plane_layer,
            vol_cols=vol_cols,
            chans=chans,
            split_out=split_out,
        ),
        out_shape=out_shape,
        in_specs=[ANYWHERE_VMEM] * (len(inputs) + 1),
        out_specs=(ANYWHERE_VMEM, ANYWHERE_VMEM) if split_out else ANYWHERE_VMEM,
    )(*in_vmem(list(inputs) + [src]))


def _half_kernel(*refs, depth_layer, plane_layer, vol_cols, chans, row_half):
    src_ref, o_ref = refs[-2:]
    if depth_layer is None:
        h = src_ref[row_half * chans : (row_half + 1) * chans, :vol_cols]
    else:
        lo_ref, mid_ref, up_ref = refs[:3]
        stacked = jnp.concatenate([lo_ref[...], mid_ref[...], up_ref[...]], axis=0)
        rows = slice(depth_layer * chans, (depth_layer + 1) * chans)
        at = vol_cols + 18 * chans
        total = jnp.dot(src_ref[rows, at : at + 3 * chans], stacked, preferred_element_type=jnp.float32)
        h = jnp.maximum(total, 0.0).astype(jnp.bfloat16)
    ok = _masks(h.shape[1])
    rows = slice(plane_layer * chans, (plane_layer + 1) * chans)
    for k in range(2):
        at = vol_cols + k * 9 * chans
        w = src_ref[rows, at : at + 9 * chans]
        h = jnp.maximum(_plane(h, w, ok), 0.0).astype(jnp.bfloat16)
    o_ref[...] = h


def half_kernel(inputs, src, vol_cols, chans, depth_layer, plane_layer, row_half=0):
    return pl.pallas_call(
        functools.partial(
            _half_kernel,
            depth_layer=depth_layer,
            plane_layer=plane_layer,
            vol_cols=vol_cols,
            chans=chans,
            row_half=row_half,
        ),
        out_shape=pltpu.VMEM((chans, vol_cols), jnp.bfloat16),
        in_specs=[ANYWHERE_VMEM] * (len(inputs) + 1),
        out_specs=ANYWHERE_VMEM,
    )(*in_vmem(list(inputs) + [src]))


def shift_z(block, step):
    size = lax.axis_size("z")
    route = [(i, i + step) for i in range(size) if 0 <= i + step < size]
    return lax.ppermute(block, "z", route)


def local(volume, plane_a, plane_b, depth):
    layers, out_part, chans = plane_a.shape[:3]
    part, slab, flat = volume.shape
    members = lax.axis_size("yh") * lax.axis_size("ch")
    per = slab // members
    vol_cols = per * flat
    sent_volume = jnp.transpose(volume.reshape(part, members, per, flat), (1, 0, 2, 3))
    sent_volume = sent_volume.reshape(members, part, vol_cols)
    weights = pack_weights(plane_a, plane_b, depth)
    mine = lax.dynamic_index_in_dim(weights, lax.axis_index("yh"), 1, keepdims=False)
    sent_weights = jnp.broadcast_to(mine[None], (members,) + mine.shape)
    sent = jnp.concatenate([sent_volume, sent_weights], axis=2)
    got = lax.all_to_all(sent, GROUP, split_axis=0, concat_axis=0, tiled=True)
    src = got.reshape(2 * chans, -1)
    high = half_kernel([], src, vol_cols, chans, None, 0, 1)
    below = shift_z(high, 1)
    low = half_kernel([], src, vol_cols, chans, None, 0, 0)
    above = shift_z(low, -1)
    for layer_index in range(layers - 1):
        new_low = half_kernel([below, low, high], src, vol_cols, chans, layer_index, layer_index + 1)
        new_high = half_kernel([low, high, above], src, vol_cols, chans, layer_index, layer_index + 1)
        low, high = new_low, new_high
        below = shift_z(high, 1)
        above = shift_z(low, -1)
    out = layer_kernel(
        [below, low, high, above], src, vol_cols, chans, layers - 1, None, False
    )
    h = lax.all_to_all(out.reshape(members, part, vol_cols), GROUP, split_axis=0, concat_axis=0, tiled=True)
    h = jnp.transpose(h.reshape(members, part, per, flat), (1, 0, 2, 3))
    return h.reshape(part, slab, flat)


def solution(mesh):
    slabs = mesh.shape["gz"]
    split = Mesh(
        mesh.devices.reshape(slabs // 4, 2, 2, mesh.shape["ch"]), ("z", "yh", "core", "ch")
    )
    return jax.shard_map(
        local,
        mesh=split,
        in_specs=(
            P("ch", SLAB, None),
            P(None, "ch", None, None, None),
            P(None, "ch", None, None, None),
            P(None, "ch", None, None),
        ),
        out_specs=P("ch", SLAB, None),
        check_vma=False,
    )
```

```python
import functools

import jax
import jax.numpy as jnp
from jax import lax
from jax.experimental import pallas as pl
from jax.experimental.pallas import tpu as pltpu
from jax.sharding import Mesh
from jax.sharding import PartitionSpec as P

X = 64
Y = 8
SLAB = ("z", "yh", "core")
GROUP = ("yh", "ch")


ANYWHERE_VMEM = pl.BlockSpec(memory_space=pltpu.VMEM)


def in_vmem(arrays):
    return [pltpu.with_memory_space_constraint(a, pltpu.VMEM) for a in arrays]


def pack_weights(plane_a, plane_b, depth):
    layers, out_part, chans = plane_a.shape[:3]
    planes = jnp.transpose(jnp.stack([plane_a, plane_b]), (2, 1, 0, 4, 5, 3))
    planes = planes.reshape(out_part, layers, 18 * chans)
    taps_d = jnp.transpose(depth, (1, 0, 3, 2)).reshape(out_part, layers, 3 * chans)
    return jnp.concatenate([planes, taps_d], axis=2)


def _masks(width):
    p = lax.broadcasted_iota(jnp.int32, (1, width), 1)
    yy = p % Y
    xx = (p // Y) % X
    xm = [xx >= 1, None, xx <= X - 2]
    ym = [yy >= 1, None, yy <= Y - 2]
    ok = []
    for a in range(3):
        row = []
        for b in range(3):
            if xm[a] is None:
                row.append(ym[b])
            elif ym[b] is None:
                row.append(xm[a])
            else:
                row.append(jnp.logical_and(xm[a], ym[b]))
        ok.append(row)
    return ok


def _plane(x, w, ok):
    width = x.shape[1]
    pieces = []
    for a in range(3):
        for b in range(3):
            d = (a - 1) * Y + (b - 1)
            moved = x if d == 0 else pltpu.roll(x, (-d) % width, 1)
            mask = ok[a][b]
            if mask is not None:
                moved = jnp.where(mask, moved, jnp.zeros_like(moved))
            pieces.append(moved)
    stacked = jnp.concatenate(pieces, axis=0)
    return jnp.dot(w, stacked, preferred_element_type=jnp.float32)


def shift_z(block, step):
    size = lax.axis_size("z")
    route = [(i, i + step) for i in range(size) if 0 <= i + step < size]
    return lax.ppermute(block, "z", route)


def _own_kernel(src_ref, o_ref, *, vol_cols, chans):
    h = jnp.concatenate([src_ref[:chans, :vol_cols], src_ref[chans:, :vol_cols]], axis=1)
    o_ref[...] = _planes(h, src_ref, 0, vol_cols, chans)


def _side_kernel(left_ref, right_ref, src_ref, o_ref, *, vol_cols, chans):
    h = jnp.concatenate(
        [left_ref[:chans], left_ref[chans:], right_ref[:chans], right_ref[chans:]], axis=1
    )
    o_ref[...] = _planes(h, src_ref, 0, vol_cols, chans)


def _planes(h, src_ref, layer, vol_cols, chans):
    ok = _masks(h.shape[1])
    rows = slice(layer * chans, (layer + 1) * chans)
    for k in range(2):
        at = vol_cols + k * 9 * chans
        w = src_ref[rows, at : at + 9 * chans]
        h = jnp.maximum(_plane(h, w, ok), 0.0).astype(jnp.bfloat16)
    return h


def _depth(parts, src_ref, layer, vol_cols, chans):
    rows = slice(layer * chans, (layer + 1) * chans)
    at = vol_cols + 18 * chans
    stacked = jnp.concatenate(parts, axis=0)
    return jnp.dot(src_ref[rows, at : at + 3 * chans], stacked, preferred_element_type=jnp.float32)


def _rest_kernel(side_ref, own_ref, keep_ref, src_ref, o_ref, *, vol_cols, chans):
    w = vol_cols
    q = [side_ref[:, :w], side_ref[:, w : 2 * w], own_ref[:, :w], own_ref[:, w:],
         side_ref[:, 2 * w : 3 * w], side_ref[:, 3 * w :]]
    total = _depth(
        [jnp.concatenate(q[0:4], axis=1), jnp.concatenate(q[1:5], axis=1), jnp.concatenate(q[2:6], axis=1)],
        src_ref, 0, vol_cols, chans,
    )
    total = jnp.where(keep_ref[...] > 0, total, 0.0)
    h = jnp.maximum(total, 0.0).astype(jnp.bfloat16)
    s = _planes(h, src_ref, 1, vol_cols, chans)
    total = _depth([s[:, : 2 * w], s[:, w : 3 * w], s[:, 2 * w :]], src_ref, 1, vol_cols, chans)
    h = jnp.maximum(total, 0.0).astype(jnp.bfloat16)
    o_ref[...] = jnp.concatenate([h[:, :w], h[:, w:]], axis=0)


def run(kernel, inputs, out_shape, **params):
    return pl.pallas_call(
        functools.partial(kernel, **params),
        out_shape=out_shape,
        in_specs=[ANYWHERE_VMEM] * len(inputs),
        out_specs=ANYWHERE_VMEM,
    )(*in_vmem(inputs))


def local(volume, plane_a, plane_b, depth):
    layers, out_part, chans = plane_a.shape[:3]
    part, slab, flat = volume.shape
    members = lax.axis_size("yh") * lax.axis_size("ch")
    per = slab // members
    vol_cols = per * flat
    sent_volume = jnp.transpose(volume.reshape(part, members, per, flat), (1, 0, 2, 3))
    sent_volume = sent_volume.reshape(members, part, vol_cols)
    weights = pack_weights(plane_a, plane_b, depth)
    mine = lax.dynamic_index_in_dim(weights, lax.axis_index("yh"), 1, keepdims=False)
    sent_weights = jnp.broadcast_to(mine[None], (members,) + mine.shape)
    sent = jnp.concatenate([sent_volume, sent_weights], axis=2)
    got = lax.all_to_all(sent, GROUP, split_axis=0, concat_axis=0, tiled=True)
    src = got.reshape(2 * chans, -1)
    raw = src[:, :vol_cols]
    left = shift_z(raw, 1)
    right = shift_z(raw, -1)
    z, last = lax.axis_index("z"), lax.axis_size("z") - 1
    lane = lax.broadcasted_iota(jnp.int32, (1, 4 * vol_cols), 1)
    outside = ((lane < vol_cols) & (z == 0)) | ((lane >= 3 * vol_cols) & (z == last))
    keep = jnp.where(outside, 0.0, 1.0).astype(jnp.float32)
    shape = functools.partial(pltpu.VMEM, dtype=jnp.bfloat16)
    own = run(_own_kernel, [src], shape((chans, 2 * vol_cols)), vol_cols=vol_cols, chans=chans)
    side = run(_side_kernel, [left, right, src], shape((chans, 4 * vol_cols)), vol_cols=vol_cols, chans=chans)
    out = run(_rest_kernel, [side, own, keep, src], shape((2 * chans, vol_cols)), vol_cols=vol_cols, chans=chans)
    h = lax.all_to_all(out.reshape(members, part, vol_cols), GROUP, split_axis=0, concat_axis=0, tiled=True)
    h = jnp.transpose(h.reshape(members, part, per, flat), (1, 0, 2, 3))
    return h.reshape(part, slab, flat)


def solution(mesh):
    slabs = mesh.shape["gz"]
    split = Mesh(
        mesh.devices.reshape(slabs // 4, 2, 2, mesh.shape["ch"]), ("z", "yh", "core", "ch")
    )
    return jax.shard_map(
        local,
        mesh=split,
        in_specs=(
            P("ch", SLAB, None),
            P(None, "ch", None, None, None),
            P(None, "ch", None, None, None),
            P(None, "ch", None, None),
        ),
        out_specs=P("ch", SLAB, None),
        check_vma=False,
    )
```

```python
import functools

import jax
import jax.numpy as jnp
from jax import lax
from jax.experimental import pallas as pl
from jax.experimental.pallas import tpu as pltpu
from jax.sharding import Mesh
from jax.sharding import PartitionSpec as P

X = 64
Y = 8
SLAB = ("z", "yh", "core")
GROUP = ("yh", "ch")


ANYWHERE_VMEM = pl.BlockSpec(memory_space=pltpu.VMEM)


def in_vmem(arrays):
    return [pltpu.with_memory_space_constraint(a, pltpu.VMEM) for a in arrays]


def pack_weights(plane_a, plane_b, depth):
    layers, out_part, chans = plane_a.shape[:3]
    planes = jnp.transpose(jnp.stack([plane_a, plane_b]), (2, 1, 0, 4, 5, 3))
    planes = planes.reshape(out_part, layers, 18 * chans)
    taps_d = jnp.transpose(depth, (1, 0, 3, 2)).reshape(out_part, layers, 3 * chans)
    return jnp.concatenate([planes, taps_d], axis=2)


def _masks(width):
    p = lax.broadcasted_iota(jnp.int32, (1, width), 1)
    yy = p % Y
    xx = (p // Y) % X
    xm = [xx >= 1, None, xx <= X - 2]
    ym = [yy >= 1, None, yy <= Y - 2]
    ok = []
    for a in range(3):
        row = []
        for b in range(3):
            if xm[a] is None:
                row.append(ym[b])
            elif ym[b] is None:
                row.append(xm[a])
            else:
                row.append(jnp.logical_and(xm[a], ym[b]))
        ok.append(row)
    return ok


def _plane(x, w, ok):
    width = x.shape[1]
    pieces = []
    for a in range(3):
        for b in range(3):
            d = (a - 1) * Y + (b - 1)
            moved = x if d == 0 else pltpu.roll(x, (-d) % width, 1)
            mask = ok[a][b]
            if mask is not None:
                moved = jnp.where(mask, moved, jnp.zeros_like(moved))
            pieces.append(moved)
    stacked = jnp.concatenate(pieces, axis=0)
    return jnp.dot(w, stacked, preferred_element_type=jnp.float32)


def shift_z(block, step):
    size = lax.axis_size("z")
    route = [(i, i + step) for i in range(size) if 0 <= i + step < size]
    return lax.ppermute(block, "z", route)


def _own_kernel(src_ref, o_ref, *, vol_cols, chans):
    h = jnp.concatenate([src_ref[:chans, :vol_cols], src_ref[chans:, :vol_cols]], axis=1)
    o_ref[...] = _planes(h, src_ref, 0, vol_cols, chans)


def _side_kernel(side_ref, src_ref, o_ref, *, vol_cols, chans):
    h = jnp.concatenate([side_ref[:chans], side_ref[chans:]], axis=1)
    o_ref[...] = _planes(h, src_ref, 0, vol_cols, chans)


def _planes(h, src_ref, layer, vol_cols, chans):
    ok = _masks(h.shape[1])
    rows = slice(layer * chans, (layer + 1) * chans)
    for k in range(2):
        at = vol_cols + k * 9 * chans
        w = src_ref[rows, at : at + 9 * chans]
        h = jnp.maximum(_plane(h, w, ok), 0.0).astype(jnp.bfloat16)
    return h


def _depth(parts, src_ref, layer, vol_cols, chans):
    rows = slice(layer * chans, (layer + 1) * chans)
    at = vol_cols + 18 * chans
    stacked = jnp.concatenate(parts, axis=0)
    return jnp.dot(src_ref[rows, at : at + 3 * chans], stacked, preferred_element_type=jnp.float32)


def _rest_kernel(left_ref, own_ref, right_ref, keep_ref, src_ref, o_ref, *, vol_cols, chans):
    w = vol_cols
    q = [left_ref[:, :w], left_ref[:, w:], own_ref[:, :w], own_ref[:, w:],
         right_ref[:, :w], right_ref[:, w:]]
    total = _depth(
        [jnp.concatenate(q[0:4], axis=1), jnp.concatenate(q[1:5], axis=1), jnp.concatenate(q[2:6], axis=1)],
        src_ref, 0, vol_cols, chans,
    )
    total = jnp.where(keep_ref[...] > 0, total, 0.0)
    h = jnp.maximum(total, 0.0).astype(jnp.bfloat16)
    s = _planes(h, src_ref, 1, vol_cols, chans)
    total = _depth([s[:, : 2 * w], s[:, w : 3 * w], s[:, 2 * w :]], src_ref, 1, vol_cols, chans)
    h = jnp.maximum(total, 0.0).astype(jnp.bfloat16)
    o_ref[...] = jnp.concatenate([h[:, :w], h[:, w:]], axis=0)


def run(kernel, inputs, out_shape, **params):
    return pl.pallas_call(
        functools.partial(kernel, **params),
        out_shape=out_shape,
        in_specs=[ANYWHERE_VMEM] * len(inputs),
        out_specs=ANYWHERE_VMEM,
    )(*in_vmem(inputs))


def local(volume, plane_a, plane_b, depth):
    layers, out_part, chans = plane_a.shape[:3]
    part, slab, flat = volume.shape
    members = lax.axis_size("yh") * lax.axis_size("ch")
    per = slab // members
    vol_cols = per * flat
    sent_volume = jnp.transpose(volume.reshape(part, members, per, flat), (1, 0, 2, 3))
    sent_volume = sent_volume.reshape(members, part, vol_cols)
    weights = pack_weights(plane_a, plane_b, depth)
    mine = lax.dynamic_index_in_dim(weights, lax.axis_index("yh"), 1, keepdims=False)
    sent_weights = jnp.broadcast_to(mine[None], (members,) + mine.shape)
    sent = jnp.concatenate([sent_volume, sent_weights], axis=2)
    got = lax.all_to_all(sent, GROUP, split_axis=0, concat_axis=0, tiled=True)
    src = got.reshape(2 * chans, -1)
    raw = src[:, :vol_cols]
    left = shift_z(raw, 1)
    right = shift_z(raw, -1)
    z, last = lax.axis_index("z"), lax.axis_size("z") - 1
    lane = lax.broadcasted_iota(jnp.int32, (1, 4 * vol_cols), 1)
    outside = ((lane < vol_cols) & (z == 0)) | ((lane >= 3 * vol_cols) & (z == last))
    keep = jnp.where(outside, 0.0, 1.0).astype(jnp.float32)
    shape = functools.partial(pltpu.VMEM, dtype=jnp.bfloat16)
    own = run(_own_kernel, [src], shape((chans, 2 * vol_cols)), vol_cols=vol_cols, chans=chans)
    pair = shape((chans, 2 * vol_cols))
    left = run(_side_kernel, [left, src], pair, vol_cols=vol_cols, chans=chans)
    right = run(_side_kernel, [right, src], pair, vol_cols=vol_cols, chans=chans)
    out = run(
        _rest_kernel, [left, own, right, keep, src], shape((2 * chans, vol_cols)),
        vol_cols=vol_cols, chans=chans,
    )
    h = lax.all_to_all(out.reshape(members, part, vol_cols), GROUP, split_axis=0, concat_axis=0, tiled=True)
    h = jnp.transpose(h.reshape(members, part, per, flat), (1, 0, 2, 3))
    return h.reshape(part, slab, flat)


def solution(mesh):
    slabs = mesh.shape["gz"]
    split = Mesh(
        mesh.devices.reshape(slabs // 4, 2, 2, mesh.shape["ch"]), ("z", "yh", "core", "ch")
    )
    return jax.shard_map(
        local,
        mesh=split,
        in_specs=(
            P("ch", SLAB, None),
            P(None, "ch", None, None, None),
            P(None, "ch", None, None, None),
            P(None, "ch", None, None),
        ),
        out_specs=P("ch", SLAB, None),
        check_vma=False,
    )
```

```python
import functools

import jax
import jax.numpy as jnp
from jax import lax
from jax.experimental import pallas as pl
from jax.experimental.pallas import tpu as pltpu
from jax.sharding import Mesh
from jax.sharding import PartitionSpec as P

X = 64
Y = 8
SLAB = ("z", "yh", "core")
GROUP = ("yh", "ch")


ANYWHERE_VMEM = pl.BlockSpec(memory_space=pltpu.VMEM)


def in_vmem(arrays):
    return [pltpu.with_memory_space_constraint(a, pltpu.VMEM) for a in arrays]


def pack_weights(plane_a, plane_b, depth):
    layers, out_part, chans = plane_a.shape[:3]
    planes = jnp.transpose(jnp.stack([plane_a, plane_b]), (2, 1, 0, 4, 5, 3))
    planes = planes.reshape(out_part, layers, 18 * chans)
    taps_d = jnp.transpose(depth, (1, 0, 3, 2)).reshape(out_part, layers, 3 * chans)
    return jnp.concatenate([planes, taps_d], axis=2)


def _masks(width):
    p = lax.broadcasted_iota(jnp.int32, (1, width), 1)
    yy = p % Y
    xx = (p // Y) % X
    xm = [xx >= 1, None, xx <= X - 2]
    ym = [yy >= 1, None, yy <= Y - 2]
    ok = []
    for a in range(3):
        row = []
        for b in range(3):
            if xm[a] is None:
                row.append(ym[b])
            elif ym[b] is None:
                row.append(xm[a])
            else:
                row.append(jnp.logical_and(xm[a], ym[b]))
        ok.append(row)
    return ok


def _plane(x, w, ok):
    width = x.shape[1]
    pieces = []
    for a in range(3):
        for b in range(3):
            d = (a - 1) * Y + (b - 1)
            moved = x if d == 0 else pltpu.roll(x, (-d) % width, 1)
            mask = ok[a][b]
            if mask is not None:
                moved = jnp.where(mask, moved, jnp.zeros_like(moved))
            pieces.append(moved)
    stacked = jnp.concatenate(pieces, axis=0)
    return jnp.dot(w, stacked, preferred_element_type=jnp.float32)


def shift_z(block, step):
    size = lax.axis_size("z")
    route = [(i, i + step) for i in range(size) if 0 <= i + step < size]
    return lax.ppermute(block, "z", route)


def _own_kernel(src_ref, o_ref, *, vol_cols, chans):
    h = jnp.concatenate([src_ref[:chans, :vol_cols], src_ref[chans:, :vol_cols]], axis=1)
    o_ref[...] = _planes(h, src_ref, 0, vol_cols, chans)


def _side_kernel(side_ref, src_ref, o_ref, *, vol_cols, chans):
    h = jnp.concatenate([side_ref[:chans], side_ref[chans:]], axis=1)
    o_ref[...] = _planes(h, src_ref, 0, vol_cols, chans)


def _planes(h, src_ref, layer, vol_cols, chans):
    ok = _masks(h.shape[1])
    rows = slice(layer * chans, (layer + 1) * chans)
    for k in range(2):
        at = vol_cols + k * 9 * chans
        w = src_ref[rows, at : at + 9 * chans]
        h = jnp.maximum(_plane(h, w, ok), 0.0).astype(jnp.bfloat16)
    return h


def _depth(parts, src_ref, layer, vol_cols, chans):
    rows = slice(layer * chans, (layer + 1) * chans)
    at = vol_cols + 18 * chans
    stacked = jnp.concatenate(parts, axis=0)
    return jnp.dot(src_ref[rows, at : at + 3 * chans], stacked, preferred_element_type=jnp.float32)


def _rest_kernel(left_ref, own_ref, right_ref, keep_ref, src_ref, o_ref, *, vol_cols, chans):
    w = vol_cols
    q = [left_ref[:, :w], left_ref[:, w:], own_ref[:, :w], own_ref[:, w:],
         right_ref[:, :w], right_ref[:, w:]]
    total = _depth(
        [jnp.concatenate(q[0:4], axis=1), jnp.concatenate(q[1:5], axis=1), jnp.concatenate(q[2:6], axis=1)],
        src_ref, 0, vol_cols, chans,
    )
    total = jnp.where(keep_ref[...] > 0, total, 0.0)
    h = jnp.maximum(total, 0.0).astype(jnp.bfloat16)
    s = _planes(h, src_ref, 1, vol_cols, chans)
    total = _depth([s[:, : 2 * w], s[:, w : 3 * w], s[:, 2 * w :]], src_ref, 1, vol_cols, chans)
    h = jnp.maximum(total, 0.0).astype(jnp.bfloat16)
    o_ref[...] = jnp.concatenate([h[:, :w], h[:, w:]], axis=0)


def run(kernel, inputs, out_shape, **params):
    return pl.pallas_call(
        functools.partial(kernel, **params),
        out_shape=out_shape,
        in_specs=[ANYWHERE_VMEM] * len(inputs),
        out_specs=ANYWHERE_VMEM,
    )(*in_vmem(inputs))


def layers_of(volume, plane_a, plane_b, depth):
    _, _, chans = plane_a.shape[:3]
    part, slab, flat = volume.shape
    members = lax.axis_size("yh") * lax.axis_size("ch")
    per = slab // members
    vol_cols = per * flat
    sent_volume = jnp.transpose(volume.reshape(part, members, per, flat), (1, 0, 2, 3))
    sent_volume = sent_volume.reshape(members, part, vol_cols)
    weights = pack_weights(plane_a, plane_b, depth)
    mine = lax.dynamic_index_in_dim(weights, lax.axis_index("yh"), 1, keepdims=False)
    sent_weights = jnp.broadcast_to(mine[None], (members,) + mine.shape)
    sent = jnp.concatenate([sent_volume, sent_weights], axis=2)
    got = lax.all_to_all(sent, GROUP, split_axis=0, concat_axis=0, tiled=True)
    src = got.reshape(2 * chans, -1)
    raw = src[:, :vol_cols]
    left = shift_z(raw, 1)
    right = shift_z(raw, -1)
    z, last = lax.axis_index("z"), lax.axis_size("z") - 1
    lane = lax.broadcasted_iota(jnp.int32, (1, 4 * vol_cols), 1)
    outside = ((lane < vol_cols) & (z == 0)) | ((lane >= 3 * vol_cols) & (z == last))
    keep = jnp.where(outside, 0.0, 1.0).astype(jnp.float32)
    shape = functools.partial(pltpu.VMEM, dtype=jnp.bfloat16)
    own = run(_own_kernel, [src], shape((chans, 2 * vol_cols)), vol_cols=vol_cols, chans=chans)
    pair = shape((chans, 2 * vol_cols))
    left = run(_side_kernel, [left, src], pair, vol_cols=vol_cols, chans=chans)
    right = run(_side_kernel, [right, src], pair, vol_cols=vol_cols, chans=chans)
    out = run(
        _rest_kernel, [left, own, right, keep, src], shape((2 * chans, vol_cols)),
        vol_cols=vol_cols, chans=chans,
    )
    h = lax.all_to_all(out.reshape(members, part, vol_cols), GROUP, split_axis=0, concat_axis=0, tiled=True)
    h = jnp.transpose(h.reshape(members, part, per, flat), (1, 0, 2, 3))
    return h.reshape(part, slab, flat)


def solution(mesh):
    slabs = mesh.shape["gz"]
    split = Mesh(
        mesh.devices.reshape(slabs // 4, 2, 2, mesh.shape["ch"]), ("z", "yh", "core", "ch")
    )
    return jax.shard_map(
        layers_of,
        mesh=split,
        in_specs=(
            P("ch", SLAB, None),
            P(None, "ch", None, None, None),
            P(None, "ch", None, None, None),
            P(None, "ch", None, None),
        ),
        out_specs=P("ch", SLAB, None),
        check_vma=False,
    )
```

```python
import functools

import jax
import jax.numpy as jnp
from jax import lax
from jax.experimental import pallas as pl
from jax.experimental.pallas import tpu as pltpu
from jax.sharding import Mesh
from jax.sharding import PartitionSpec as P

X = 64
Y = 8
SLAB = ("z", "yh", "core")
GROUP = ("yh", "ch")


ANYWHERE_VMEM = pl.BlockSpec(memory_space=pltpu.VMEM)


def in_vmem(arrays):
    return [pltpu.with_memory_space_constraint(a, pltpu.VMEM) for a in arrays]


def pack_weights(plane_a, plane_b, depth):
    layers, out_part, chans = plane_a.shape[:3]
    planes = jnp.transpose(jnp.stack([plane_a, plane_b]), (2, 1, 0, 4, 5, 3))
    planes = planes.reshape(out_part, layers, 18 * chans)
    taps_d = jnp.transpose(depth, (1, 0, 3, 2)).reshape(out_part, layers, 3 * chans)
    return jnp.concatenate([planes, taps_d], axis=2)


def _masks(width):
    p = lax.broadcasted_iota(jnp.int32, (1, width), 1)
    yy = p % Y
    xx = (p // Y) % X
    xm = [xx >= 1, None, xx <= X - 2]
    ym = [yy >= 1, None, yy <= Y - 2]
    ok = []
    for a in range(3):
        row = []
        for b in range(3):
            if xm[a] is None:
                row.append(ym[b])
            elif ym[b] is None:
                row.append(xm[a])
            else:
                row.append(jnp.logical_and(xm[a], ym[b]))
        ok.append(row)
    return ok


def _plane(x, w, ok):
    width = x.shape[1]
    pieces = []
    for a in range(3):
        for b in range(3):
            d = (a - 1) * Y + (b - 1)
            moved = x if d == 0 else pltpu.roll(x, (-d) % width, 1)
            mask = ok[a][b]
            if mask is not None:
                moved = jnp.where(mask, moved, jnp.zeros_like(moved))
            pieces.append(moved)
    stacked = jnp.concatenate(pieces, axis=0)
    return jnp.dot(w, stacked, preferred_element_type=jnp.float32)


def shift_z(block, step):
    size = lax.axis_size("z")
    route = [(i, i + step) for i in range(size) if 0 <= i + step < size]
    return lax.ppermute(block, "z", route)


def _own_kernel(src_ref, o_ref, *, vol_cols, chans):
    h = jnp.concatenate([src_ref[:chans, :vol_cols], src_ref[chans:, :vol_cols]], axis=1)
    o_ref[...] = _planes(h, src_ref, 0, vol_cols, chans)


def _side_kernel(side_ref, src_ref, o_ref, *, vol_cols, chans):
    h = jnp.concatenate([side_ref[:chans], side_ref[chans:]], axis=1)
    o_ref[...] = _planes(h, src_ref, 0, vol_cols, chans)


def _planes(h, src_ref, layer, vol_cols, chans):
    ok = _masks(h.shape[1])
    rows = slice(layer * chans, (layer + 1) * chans)
    for k in range(2):
        at = vol_cols + k * 9 * chans
        w = src_ref[rows, at : at + 9 * chans]
        h = jnp.maximum(_plane(h, w, ok), 0.0).astype(jnp.bfloat16)
    return h


def _depth(parts, src_ref, layer, vol_cols, chans):
    rows = slice(layer * chans, (layer + 1) * chans)
    at = vol_cols + 18 * chans
    stacked = jnp.concatenate(parts, axis=0)
    return jnp.dot(src_ref[rows, at : at + 3 * chans], stacked, preferred_element_type=jnp.float32)


def _rest_kernel(left_ref, own_ref, right_ref, src_ref, o_ref, *, vol_cols, chans):
    w = vol_cols
    q = [left_ref[:, :w], left_ref[:, w:], own_ref[:, :w], own_ref[:, w:],
         right_ref[:, :w], right_ref[:, w:]]
    total = _depth(
        [jnp.concatenate(q[0:4], axis=1), jnp.concatenate(q[1:5], axis=1), jnp.concatenate(q[2:6], axis=1)],
        src_ref, 0, vol_cols, chans,
    )
    z, last = lax.axis_index("z"), lax.axis_size("z") - 1
    lane = lax.broadcasted_iota(jnp.int32, (1, 4 * w), 1)
    outside = jnp.logical_or(
        jnp.logical_and(lane < w, z == 0), jnp.logical_and(lane >= 3 * w, z == last)
    )
    total = jnp.where(outside, 0.0, total)
    h = jnp.maximum(total, 0.0).astype(jnp.bfloat16)
    s = _planes(h, src_ref, 1, vol_cols, chans)
    total = _depth([s[:, : 2 * w], s[:, w : 3 * w], s[:, 2 * w :]], src_ref, 1, vol_cols, chans)
    h = jnp.maximum(total, 0.0).astype(jnp.bfloat16)
    o_ref[...] = jnp.concatenate([h[:, :w], h[:, w:]], axis=0)


def run(kernel, inputs, out_shape, **params):
    return pl.pallas_call(
        functools.partial(kernel, **params),
        out_shape=out_shape,
        in_specs=[ANYWHERE_VMEM] * len(inputs),
        out_specs=ANYWHERE_VMEM,
    )(*in_vmem(inputs))


def local(volume, plane_a, plane_b, depth):
    layers, out_part, chans = plane_a.shape[:3]
    part, slab, flat = volume.shape
    members = lax.axis_size("yh") * lax.axis_size("ch")
    per = slab // members
    vol_cols = per * flat
    sent_volume = jnp.transpose(volume.reshape(part, members, per, flat), (1, 0, 2, 3))
    sent_volume = sent_volume.reshape(members, part, vol_cols)
    weights = pack_weights(plane_a, plane_b, depth)
    mine = lax.dynamic_index_in_dim(weights, lax.axis_index("yh"), 1, keepdims=False)
    sent_weights = jnp.broadcast_to(mine[None], (members,) + mine.shape)
    sent = jnp.concatenate([sent_volume, sent_weights], axis=2)
    got = lax.all_to_all(sent, GROUP, split_axis=0, concat_axis=0, tiled=True)
    src = got.reshape(2 * chans, -1)
    raw = src[:, :vol_cols]
    left = shift_z(raw, 1)
    right = shift_z(raw, -1)
    shape = functools.partial(pltpu.VMEM, dtype=jnp.bfloat16)
    own = run(_own_kernel, [src], shape((chans, 2 * vol_cols)), vol_cols=vol_cols, chans=chans)
    pair = shape((chans, 2 * vol_cols))
    left = run(_side_kernel, [left, src], pair, vol_cols=vol_cols, chans=chans)
    right = run(_side_kernel, [right, src], pair, vol_cols=vol_cols, chans=chans)
    out = run(
        _rest_kernel, [left, own, right, src], shape((2 * chans, vol_cols)),
        vol_cols=vol_cols, chans=chans,
    )
    h = lax.all_to_all(out.reshape(members, part, vol_cols), GROUP, split_axis=0, concat_axis=0, tiled=True)
    h = jnp.transpose(h.reshape(members, part, per, flat), (1, 0, 2, 3))
    return h.reshape(part, slab, flat)


def solution(mesh):
    slabs = mesh.shape["gz"]
    split = Mesh(
        mesh.devices.reshape(slabs // 4, 2, 2, mesh.shape["ch"]), ("z", "yh", "core", "ch")
    )
    return jax.shard_map(
        local,
        mesh=split,
        in_specs=(
            P("ch", SLAB, None),
            P(None, "ch", None, None, None),
            P(None, "ch", None, None, None),
            P(None, "ch", None, None),
        ),
        out_specs=P("ch", SLAB, None),
        check_vma=False,
    )
```

```python
import functools

import jax
import jax.numpy as jnp
from jax import lax
from jax.experimental import pallas as pl
from jax.experimental.pallas import tpu as pltpu
from jax.sharding import Mesh
from jax.sharding import PartitionSpec as P

X = 64
Y = 8
SLAB = ("z", "yh", "core")
GROUP = ("yh", "ch")


ANYWHERE_VMEM = pl.BlockSpec(memory_space=pltpu.VMEM)


def in_vmem(arrays):
    return [pltpu.with_memory_space_constraint(a, pltpu.VMEM) for a in arrays]


def pack_weights(plane_a, plane_b, depth):
    layers, out_part, chans = plane_a.shape[:3]
    planes = jnp.transpose(jnp.stack([plane_a, plane_b]), (2, 1, 0, 4, 5, 3))
    planes = planes.reshape(out_part, layers, 18 * chans)
    taps_d = jnp.transpose(depth, (1, 0, 3, 2)).reshape(out_part, layers, 3 * chans)
    return jnp.concatenate([planes, taps_d], axis=2)


def _masks(width):
    p = lax.broadcasted_iota(jnp.int32, (1, width), 1)
    yy = p % Y
    xx = (p // Y) % X
    xm = [xx >= 1, None, xx <= X - 2]
    ym = [yy >= 1, None, yy <= Y - 2]
    ok = []
    for a in range(3):
        row = []
        for b in range(3):
            if xm[a] is None:
                row.append(ym[b])
            elif ym[b] is None:
                row.append(xm[a])
            else:
                row.append(jnp.logical_and(xm[a], ym[b]))
        ok.append(row)
    return ok


def _plane(x, w, ok):
    width = x.shape[1]
    pieces = []
    for a in range(3):
        for b in range(3):
            d = (a - 1) * Y + (b - 1)
            moved = x if d == 0 else pltpu.roll(x, (-d) % width, 1)
            mask = ok[a][b]
            if mask is not None:
                moved = jnp.where(mask, moved, jnp.zeros_like(moved))
            pieces.append(moved)
    stacked = jnp.concatenate(pieces, axis=0)
    return jnp.dot(w, stacked, preferred_element_type=jnp.float32)


def shift_z(block, step):
    size = lax.axis_size("z")
    route = [(i, i + step) for i in range(size) if 0 <= i + step < size]
    return lax.ppermute(block, "z", route)


def _own_kernel(src_ref, o_ref, *, vol_cols, chans):
    h = jnp.concatenate([src_ref[:chans, :vol_cols], src_ref[chans:, :vol_cols]], axis=1)
    o_ref[...] = _planes(h, src_ref, 0, vol_cols, chans)


def _side_kernel(side_ref, src_ref, o_ref, *, vol_cols, chans):
    h = jnp.concatenate([side_ref[:chans], side_ref[chans:]], axis=1)
    o_ref[...] = _planes(h, src_ref, 0, vol_cols, chans)


def _planes(h, src_ref, layer, vol_cols, chans):
    ok = _masks(h.shape[1])
    rows = slice(layer * chans, (layer + 1) * chans)
    for k in range(2):
        at = vol_cols + k * 9 * chans
        w = src_ref[rows, at : at + 9 * chans]
        h = jnp.maximum(_plane(h, w, ok), 0.0).astype(jnp.bfloat16)
    return h


def _depth(parts, src_ref, layer, vol_cols, chans):
    rows = slice(layer * chans, (layer + 1) * chans)
    at = vol_cols + 18 * chans
    stacked = jnp.concatenate(parts, axis=0)
    return jnp.dot(src_ref[rows, at : at + 3 * chans], stacked, preferred_element_type=jnp.float32)


def _rest_kernel(side_ref, own_ref, right_ref, src_ref, o_ref, *, vol_cols, chans):
    w = vol_cols
    left = _planes(
        jnp.concatenate([side_ref[:chans], side_ref[chans:]], axis=1), src_ref, 0, vol_cols, chans
    )
    q = [left[:, :w], left[:, w:], own_ref[:, :w], own_ref[:, w:],
         right_ref[:, :w], right_ref[:, w:]]
    total = _depth(
        [jnp.concatenate(q[0:4], axis=1), jnp.concatenate(q[1:5], axis=1), jnp.concatenate(q[2:6], axis=1)],
        src_ref, 0, vol_cols, chans,
    )
    z, last = lax.axis_index("z"), lax.axis_size("z") - 1
    lane = lax.broadcasted_iota(jnp.int32, (1, 4 * w), 1)
    outside = jnp.logical_or(
        jnp.logical_and(lane < w, z == 0), jnp.logical_and(lane >= 3 * w, z == last)
    )
    total = jnp.where(outside, 0.0, total)
    h = jnp.maximum(total, 0.0).astype(jnp.bfloat16)
    s = _planes(h, src_ref, 1, vol_cols, chans)
    total = _depth([s[:, : 2 * w], s[:, w : 3 * w], s[:, 2 * w :]], src_ref, 1, vol_cols, chans)
    h = jnp.maximum(total, 0.0).astype(jnp.bfloat16)
    o_ref[...] = jnp.concatenate([h[:, :w], h[:, w:]], axis=0)


def run(kernel, inputs, out_shape, **params):
    return pl.pallas_call(
        functools.partial(kernel, **params),
        out_shape=out_shape,
        in_specs=[ANYWHERE_VMEM] * len(inputs),
        out_specs=ANYWHERE_VMEM,
    )(*in_vmem(inputs))


def local(volume, plane_a, plane_b, depth):
    layers, out_part, chans = plane_a.shape[:3]
    part, slab, flat = volume.shape
    members = lax.axis_size("yh") * lax.axis_size("ch")
    per = slab // members
    vol_cols = per * flat
    sent_volume = jnp.transpose(volume.reshape(part, members, per, flat), (1, 0, 2, 3))
    sent_volume = sent_volume.reshape(members, part, vol_cols)
    weights = pack_weights(plane_a, plane_b, depth)
    mine = lax.dynamic_index_in_dim(weights, lax.axis_index("yh"), 1, keepdims=False)
    sent_weights = jnp.broadcast_to(mine[None], (members,) + mine.shape)
    sent = jnp.concatenate([sent_volume, sent_weights], axis=2)
    got = lax.all_to_all(sent, GROUP, split_axis=0, concat_axis=0, tiled=True)
    src = got.reshape(2 * chans, -1)
    raw = src[:, :vol_cols]
    left = shift_z(raw, 1)
    right = shift_z(raw, -1)
    shape = functools.partial(pltpu.VMEM, dtype=jnp.bfloat16)
    own = run(_own_kernel, [src], shape((chans, 2 * vol_cols)), vol_cols=vol_cols, chans=chans)
    pair = shape((chans, 2 * vol_cols))
    right = run(_side_kernel, [right, src], pair, vol_cols=vol_cols, chans=chans)
    out = run(
        _rest_kernel, [left, own, right, src], shape((2 * chans, vol_cols)),
        vol_cols=vol_cols, chans=chans,
    )
    h = lax.all_to_all(out.reshape(members, part, vol_cols), GROUP, split_axis=0, concat_axis=0, tiled=True)
    h = jnp.transpose(h.reshape(members, part, per, flat), (1, 0, 2, 3))
    return h.reshape(part, slab, flat)


def solution(mesh):
    slabs = mesh.shape["gz"]
    split = Mesh(
        mesh.devices.reshape(slabs // 4, 2, 2, mesh.shape["ch"]), ("z", "yh", "core", "ch")
    )
    return jax.shard_map(
        local,
        mesh=split,
        in_specs=(
            P("ch", SLAB, None),
            P(None, "ch", None, None, None),
            P(None, "ch", None, None, None),
            P(None, "ch", None, None),
        ),
        out_specs=P("ch", SLAB, None),
        check_vma=False,
    )
```

```python
import functools

import jax
import jax.numpy as jnp
from jax import lax
from jax.experimental import pallas as pl
from jax.experimental.pallas import tpu as pltpu
from jax.sharding import Mesh
from jax.sharding import PartitionSpec as P

X = 64
Y = 8
SLAB = ("z", "yh", "core")
GROUP = ("yh", "ch")


ANYWHERE_VMEM = pl.BlockSpec(memory_space=pltpu.VMEM)


def in_vmem(arrays):
    return [pltpu.with_memory_space_constraint(a, pltpu.VMEM) for a in arrays]


def pack_weights(plane_a, plane_b, depth):
    layers, out_part, chans = plane_a.shape[:3]
    planes = jnp.transpose(jnp.stack([plane_a, plane_b]), (2, 1, 0, 4, 5, 3))
    planes = planes.reshape(out_part, layers, 18 * chans)
    taps_d = jnp.transpose(depth, (1, 0, 3, 2)).reshape(out_part, layers, 3 * chans)
    return jnp.concatenate([planes, taps_d], axis=2)


def _masks(width):
    p = lax.broadcasted_iota(jnp.int32, (1, width), 1)
    yy = p % Y
    xx = (p // Y) % X
    xm = [xx >= 1, None, xx <= X - 2]
    ym = [yy >= 1, None, yy <= Y - 2]
    ok = []
    for a in range(3):
        row = []
        for b in range(3):
            if xm[a] is None:
                row.append(ym[b])
            elif ym[b] is None:
                row.append(xm[a])
            else:
                row.append(jnp.logical_and(xm[a], ym[b]))
        ok.append(row)
    return ok


def _plane(x, w, ok):
    width = x.shape[1]
    pieces = []
    for a in range(3):
        for b in range(3):
            d = (a - 1) * Y + (b - 1)
            moved = x if d == 0 else pltpu.roll(x, (-d) % width, 1)
            mask = ok[a][b]
            if mask is not None:
                moved = jnp.where(mask, moved, jnp.zeros_like(moved))
            pieces.append(moved)
    stacked = jnp.concatenate(pieces, axis=0)
    return jnp.dot(w, stacked, preferred_element_type=jnp.float32)


def shift_z(block, step):
    size = lax.axis_size("z")
    route = [(i, i + step) for i in range(size) if 0 <= i + step < size]
    return lax.ppermute(block, "z", route)


def _own_kernel(src_ref, o_ref, *, vol_cols, chans):
    h = jnp.concatenate([src_ref[:chans, :vol_cols], src_ref[chans:, :vol_cols]], axis=1)
    o_ref[...] = _planes(h, src_ref, 0, vol_cols, chans)


def _side_kernel(side_ref, src_ref, o_ref, *, vol_cols, chans):
    h = jnp.concatenate([side_ref[:chans], side_ref[chans:]], axis=1)
    o_ref[...] = _planes(h, src_ref, 0, vol_cols, chans)


def _planes(h, src_ref, layer, vol_cols, chans):
    ok = _masks(h.shape[1])
    rows = slice(layer * chans, (layer + 1) * chans)
    for k in range(2):
        at = vol_cols + k * 9 * chans
        w = src_ref[rows, at : at + 9 * chans]
        h = jnp.maximum(_plane(h, w, ok), 0.0).astype(jnp.bfloat16)
    return h


def _depth(parts, src_ref, layer, vol_cols, chans):
    rows = slice(layer * chans, (layer + 1) * chans)
    at = vol_cols + 18 * chans
    stacked = jnp.concatenate(parts, axis=0)
    return jnp.dot(src_ref[rows, at : at + 3 * chans], stacked, preferred_element_type=jnp.float32)


def _rest_kernel(left_ref, own_ref, right_ref, src_ref, o_ref, *, vol_cols, chans):
    w = vol_cols
    q = [left_ref[:, :w], left_ref[:, w:], own_ref[:, :w], own_ref[:, w:],
         right_ref[:, :w], right_ref[:, w:]]
    total = _depth(
        [jnp.concatenate(q[0:4], axis=1), jnp.concatenate(q[1:5], axis=1), jnp.concatenate(q[2:6], axis=1)],
        src_ref, 0, vol_cols, chans,
    )
    z, last = lax.axis_index("z"), lax.axis_size("z") - 1
    lane = lax.broadcasted_iota(jnp.int32, (1, 4 * w), 1)
    outside = jnp.logical_or(
        jnp.logical_and(lane < w, z == 0), jnp.logical_and(lane >= 3 * w, z == last)
    )
    total = jnp.where(outside, 0.0, total)
    h = jnp.maximum(total, 0.0).astype(jnp.bfloat16)
    s = _planes(h, src_ref, 1, vol_cols, chans)
    total = _depth([s[:, : 2 * w], s[:, w : 3 * w], s[:, 2 * w :]], src_ref, 1, vol_cols, chans)
    h = jnp.maximum(total, 0.0).astype(jnp.bfloat16)
    o_ref[...] = jnp.concatenate([h[:, :w], h[:, w:]], axis=0)


def _place_kernel(h_ref, o_ref, *, per, flat):
    for m in range(h_ref.shape[0]):
        for r in range(per):
            o_ref[:, m * per + r, :] = h_ref[m, :, r * flat : (r + 1) * flat]


def run(kernel, inputs, out_shape, **params):
    return pl.pallas_call(
        functools.partial(kernel, **params),
        out_shape=out_shape,
        in_specs=[ANYWHERE_VMEM] * len(inputs),
        out_specs=ANYWHERE_VMEM,
    )(*in_vmem(inputs))


def local(volume, plane_a, plane_b, depth):
    layers, out_part, chans = plane_a.shape[:3]
    part, slab, flat = volume.shape
    members = lax.axis_size("yh") * lax.axis_size("ch")
    per = slab // members
    vol_cols = per * flat
    sent_volume = jnp.transpose(volume.reshape(part, members, per, flat), (1, 0, 2, 3))
    sent_volume = sent_volume.reshape(members, part, vol_cols)
    weights = pack_weights(plane_a, plane_b, depth)
    mine = lax.dynamic_index_in_dim(weights, lax.axis_index("yh"), 1, keepdims=False)
    sent_weights = jnp.broadcast_to(mine[None], (members,) + mine.shape)
    sent = jnp.concatenate([sent_volume, sent_weights], axis=2)
    got = lax.all_to_all(sent, GROUP, split_axis=0, concat_axis=0, tiled=True)
    src = got.reshape(2 * chans, -1)
    raw = src[:, :vol_cols]
    left = shift_z(raw, 1)
    right = shift_z(raw, -1)
    shape = functools.partial(pltpu.VMEM, dtype=jnp.bfloat16)
    own = run(_own_kernel, [src], shape((chans, 2 * vol_cols)), vol_cols=vol_cols, chans=chans)
    pair = shape((chans, 2 * vol_cols))
    left = run(_side_kernel, [left, src], pair, vol_cols=vol_cols, chans=chans)
    right = run(_side_kernel, [right, src], pair, vol_cols=vol_cols, chans=chans)
    out = run(
        _rest_kernel, [left, own, right, src], shape((2 * chans, vol_cols)),
        vol_cols=vol_cols, chans=chans,
    )
    h = lax.all_to_all(out.reshape(members, part, vol_cols), GROUP, split_axis=0, concat_axis=0, tiled=True)
    return pl.pallas_call(
        functools.partial(_place_kernel, per=per, flat=flat),
        out_shape=jax.ShapeDtypeStruct((part, slab, flat), jnp.bfloat16),
        in_specs=[ANYWHERE_VMEM],
    )(*in_vmem([h]))


def solution(mesh):
    slabs = mesh.shape["gz"]
    split = Mesh(
        mesh.devices.reshape(slabs // 4, 2, 2, mesh.shape["ch"]), ("z", "yh", "core", "ch")
    )
    return jax.shard_map(
        local,
        mesh=split,
        in_specs=(
            P("ch", SLAB, None),
            P(None, "ch", None, None, None),
            P(None, "ch", None, None, None),
            P(None, "ch", None, None),
        ),
        out_specs=P("ch", SLAB, None),
        check_vma=False,
    )
```
